32 devices in a mesh: grp: 4 (over y, x), dev: 8 (over z, core).
Axes of the slice: x: 2, y: 2, z: 4, core: 2. Of those that a mesh axis runs over, the one named last changes fastest.
Arguments:
- panel_nodes: float32 [3, 262144], P(None, ('grp', 'dev')), may hold values from -1.6 to 1.6, as said below
- density: float32 [262144], P(('grp', 'dev')), may hold values from -6 to 6
- crevice_routes: int32 [16384, 2], P(('grp', 'dev')), may hold values from 0 to 31, all different within a row; in each aligned block of 512 rows (0 to 511, 512 to 1023, ...) at most 64 rows name the same one
- crevice_centre: int32 [16384, 2], P(('grp', 'dev')), may hold values from 0 to 511
- centres: float32 [3, 16384], P(None, ('grp', 'dev')), may hold values from -0.3 to 0.3, as said below
- targets: float32 [3, 262144], P(None, ('grp', 'dev')), may hold values from -0.8 to 0.8, as said below
- centre_home: int32 [16384, 1], P(('grp', 'dev')), may hold values from 0 to 31; in each aligned block of 512 rows (0 to 511, 512 to 1023, ...) at most 32 rows name the same one
- upsample: float32 [64, 16], replicated, may hold values from 0 to 1, as said below
- fine_weights: float32 [64], replicated, may hold values from 0.005 to 0.05
Outputs:
- returned: float32 [524288], P(('grp', 'dev'))
The draws below stay inside these ranges and needn't reach their ends.
Inputs may be any that keep to these rules, and one draw needn't show every extreme that they name: `crevice_routes`: each device's 512 panels name at most 64 (panel, route) pairs for any one owner device, and some owner reaches 64 in every draw; the 2 owners of one panel differ. `centre_home`: among the 512 centres of one device at most 32 have the same home, and that bound is reached in every draw; entries of returned with no centre are zero. `panel_nodes`: every point in the convex hull of one panel's nodes lies at distance 0.9 or more from the anchor; every panel node lies within 1.6 of the anchor. `centres`: every centre lies within 0.3 of the anchor. `targets`: each target node lies at distance 0.3 to 0.5 from its centre. `upsample`: entries are positive and each row sums to one.
All inputs are finite; a program needn't handle non-finite values.
Results may differ from the reference program's by a relative error of at most 0.0003.
Values sent between devices are 32-bit elements; how exact they have to be, the bound alone decides.
No kernel may reach another device: no remote copies, remote signals or barrier semaphores. Data moves between devices by JAX's collectives and lax.ppermute only.
A program may use at most 64 MiB of HBM per device.

```python
import math
import jax
import jax.numpy as jnp
import numpy as np
from jax import lax

NODES = 16
FINE = 64
ORDER = 8
TOP = 2
P_DEV = 512
C_DEV = 512
PANELS = 16384
CENTRES = 16384
MOST = 64
MOST_BACK = 32
DEVICES = 32


def centre_positions(key):
    return jax.random.uniform(jax.random.fold_in(key, 11), (3, CENTRES), jnp.float32, -0.17, 0.17)


def directions(key, count):
    first, second = jax.random.split(key)
    height = jax.random.uniform(first, (count,), jnp.float32, -1.0, 1.0)
    angle = jax.random.uniform(second, (count,), jnp.float32, -3.14159265, 3.14159265)
    across = jnp.sqrt(1.0 - height * height)
    return jnp.stack([across * jnp.cos(angle), across * jnp.sin(angle), height])


def surface_frame(key, count):
    first, second = jax.random.split(key)
    height = jax.random.uniform(first, (count,), jnp.float32, -1.0, 1.0)
    angle = jax.random.uniform(second, (count,), jnp.float32, -3.14159265, 3.14159265)
    across = jnp.sqrt(1.0 - height * height)
    outward = jnp.stack([across * jnp.cos(angle), across * jnp.sin(angle), height])
    first_side = jnp.stack([-jnp.sin(angle), jnp.cos(angle), jnp.zeros_like(angle)])
    second_side = jnp.stack([height * jnp.cos(angle), height * jnp.sin(angle), -across])
    return (outward, first_side, second_side)


def draw_panel_nodes(key, part):
    first, second, third, fourth = jax.random.split(key, 4)
    radius = jax.random.uniform(first, (PANELS,), jnp.float32, 0.9, 1.2)
    along = jax.random.uniform(third, (2, PANELS, NODES), jnp.float32, -0.7, 0.7)
    lift = jax.random.uniform(fourth, (PANELS, NODES), jnp.float32, 0.0, 0.05)
    outward, first_side, second_side = surface_frame(second, PANELS)
    height = radius[:, None] + lift
    nodes = outward[:, :, None] * height[None, :, :] + first_side[:, :, None] * along[0][None, :, :] + second_side[:, :, None] * along[1][None, :, :]
    return nodes.reshape(3, PANELS * NODES).astype(jnp.float32)


def draw_centres(key, part):
    return centre_positions(key)


def draw_targets(key, part):
    middle = centre_positions(key)
    first, second = jax.random.split(jax.random.fold_in(key, 23))
    radius = jax.random.uniform(first, (CENTRES * NODES,), jnp.float32, 0.3, 0.5)
    offset = directions(second, CENTRES * NODES) * radius[None, :]
    return (jnp.repeat(middle, NODES, axis=1) + offset).astype(jnp.float32)


def draw_upsample(key, part):
    first, second = jax.random.split(jax.random.fold_in(key, 31))
    base = 0.1 * jax.random.uniform(first, (FINE, NODES), jnp.float32, 0.05, 1.0) ** 6
    peak = jax.random.uniform(second, (FINE, 1), jnp.float32, 0.6, 1.0)
    nearest = (jnp.arange(FINE, dtype=jnp.int32) % NODES)[:, None] == jnp.arange(NODES, dtype=jnp.int32)[None, :]
    raw = base + jnp.where(nearest, peak, 0.0)
    return (raw / jnp.sum(raw, axis=1, keepdims=True)).astype(jnp.float32)


def place_ends(result, stream_key, low, largest):
    longest = result.shape.index(max(result.shape))
    spots = []
    for shift in (0, 1):
        where = [jax.random.randint(jax.random.fold_in(stream_key, axis), (), 0, length) for axis, length in enumerate(result.shape)]
        where[longest] = (where[longest] + shift) % result.shape[longest]
        spots.append(tuple(where))
    return result.at[spots[0]].set(low).at[spots[1]].set(largest)


def steps_of(stream_key, shape, cuts, least, top_value):
    gain = 1.0
    for axis_at, shards_of in cuts:
        heights = jax.random.uniform(jax.random.fold_in(jax.random.fold_in(stream_key, 6), axis_at), (shards_of,), jnp.float32, least / len(cuts), top_value / len(cuts))
        gain = gain * jnp.repeat(jnp.exp(heights), shape[axis_at] // shards_of).reshape((-1,) + (1,) * (len(shape) - 1 - axis_at))
    return gain


def assign_block(stream_key, own, number, rows, count, top, reach, lean):
    sequence = jax.random.permutation(stream_key, count)
    packed, usual = shares(count, rows * top, reach, lean, True), shares(count, rows * top, reach, lean, False)
    places = jnp.arange(count)

    def named(lengths, offset_by):
        used = int((lengths > 0).sum())
        fixed = max(1, used // 4)
        passed = fixed + (places - fixed + offset_by * (used - fixed)) % max(1, count - fixed)
        return jnp.zeros((count,), jnp.int32).at[sequence[jnp.where(places < fixed, places, passed)]].set(jnp.asarray(lengths, jnp.int32))

    lengths = jnp.where(number % 4 == 0, named(packed, number // 4), named(usual, number - number // 4 - 1))
    mixed = jax.random.permutation(jax.random.fold_in(own, 3), count)
    source_of, taker = mixed[0:count // 2 * 2:2], mixed[1:count // 2 * 2:2]
    slack = jnp.minimum(lengths[source_of] - 1, reach - lengths[taker]) // 2
    slack = jnp.where((source_of == sequence[0]) | (taker == sequence[0]) | (lengths[taker] == 0), 0, jnp.maximum(slack, 0))
    passed = jax.random.randint(jax.random.fold_in(own, 4), (count // 2,), 0, 1 << 20) % (slack + 1)
    lengths = lengths.at[source_of].add(-passed).at[taker].add(passed)
    members = jnp.searchsorted(jnp.cumsum(lengths), jnp.arange(rows * top), side="right").astype(jnp.int32)
    grid = members.reshape(top, rows).T
    grid = grid[jax.random.permutation(jax.random.fold_in(own, 1), rows)]
    offset_by = jax.random.randint(jax.random.fold_in(own, 2), (rows, 1), 0, top)
    return jnp.take_along_axis(grid, (jnp.arange(top)[None, :] + offset_by) % top, axis=1)


def shares(amount, total, reach, lean, full):
    weights = [(1 << 20) // math.isqrt(rank ** lean) + 1 for rank in range(1, amount + 1)]
    largest = reach if full else min(reach, max(-(-total // amount), total * weights[0] // sum(weights)))
    least = 1 if total - largest >= amount - 1 else 0
    given, rest = [largest] + [least] * (amount - 1), total - largest - least * (amount - 1)
    while rest > 0:
        candidates = [i for i in range(1, amount) if given[i] < largest] or [i for i in range(1, amount) if given[i] < reach]
        whole, left = sum([weights[i] for i in candidates]), rest
        for i in candidates:
            more = min(reach - given[i], max(1, left * weights[i] // whole), rest)
            given[i] = given[i] + more
            rest = rest - more
    return np.array(given)


def centred(key, extent, spread, reach, cuts=(), kind=jnp.bfloat16):
    result = spread * jax.random.normal(key, extent, jnp.float32)
    if cuts:
        result = result * steps_of(key, extent, cuts, -0.22, 0.18)
    return jnp.clip(result, -reach, reach).astype(kind)


def setup_inputs(seed: int = 0) -> dict:
    keys = jax.random.split(jax.random.key(seed), 10)
    panel_nodes = draw_panel_nodes(jax.random.fold_in(keys[9], 71), 0)
    density = centred(keys[1], (PANELS * NODES,), 1.0, 6.0, ((0, 32),), jnp.float32)
    crevice_routes_keys = jax.random.split(jax.random.fold_in(keys[2], 1), PANELS // P_DEV)
    crevice_routes_turns = jax.random.permutation(jax.random.fold_in(keys[2], 3), PANELS // P_DEV)
    crevice_routes = jax.vmap(lambda own, number: assign_block(jax.random.fold_in(keys[2], 2), own, number, P_DEV, DEVICES, TOP, MOST, 2))(crevice_routes_keys, crevice_routes_turns).reshape((PANELS, TOP))
    crevice_centre = place_ends(jax.random.randint(keys[3], (PANELS, TOP), 0, C_DEV), jax.random.fold_in(keys[3], 1), 0, C_DEV - 1).astype(jnp.int32)
    centres = draw_centres(jax.random.fold_in(keys[9], 71), 0)
    targets = draw_targets(jax.random.fold_in(keys[9], 71), 0)
    centre_home_keys = jax.random.split(jax.random.fold_in(keys[6], 1), CENTRES // C_DEV)
    centre_home_turns = jax.random.permutation(jax.random.fold_in(keys[6], 3), CENTRES // C_DEV)
    centre_home = jax.vmap(lambda own, number: assign_block(jax.random.fold_in(keys[6], 2), own, number, C_DEV, DEVICES, 1, MOST_BACK, 1))(centre_home_keys, centre_home_turns).reshape((CENTRES, 1))
    upsample = draw_upsample(jax.random.fold_in(keys[9], 71), 0)
    fine_weights = jnp.clip(jnp.exp(jax.random.uniform(keys[8], (FINE,), jnp.float32, math.log(0.005), math.log(0.05))), 0.005, 0.05)
    return {"panel_nodes": panel_nodes, "density": density, "crevice_routes": crevice_routes, "crevice_centre": crevice_centre, "centres": centres, "targets": targets, "centre_home": centre_home, "upsample": upsample, "fine_weights": fine_weights}


def route_rank(destination, count):
    onehot = (destination[:, None] == jnp.arange(count, dtype=jnp.int32)[None, :]).astype(jnp.int32)
    before = jnp.cumsum(onehot, axis=0) - onehot
    return lax.optimization_barrier(jnp.sum(before * onehot, axis=1)).astype(jnp.int32)

def refine(coarse_all, upsample, fine_weights):
    upper = jnp.einsum('sck,nk->scn', coarse_all, upsample, precision=lax.Precision.HIGHEST)
    strength = upper[:, 3, :] * fine_weights[None, :]
    return jnp.concatenate([upper[:, :3, :], strength[:, None, :]], axis=1)

def expansion_terms(sources, centre_pos, target_pos):
    src_vec = sources[:, :3, :] - centre_pos[:, :, None]
    tgt_vec = target_pos - centre_pos[:, :, None]
    src_dist = jnp.sqrt(lax.optimization_barrier(jnp.sum(src_vec * src_vec, axis=1)))
    tgt_dist = jnp.sqrt(lax.optimization_barrier(jnp.sum(tgt_vec * tgt_vec, axis=1)))
    inner = lax.optimization_barrier(jnp.sum(src_vec[:, :, :, None] * tgt_vec[:, :, None, :], axis=1))
    cosine = inner / (src_dist[:, :, None] * tgt_dist[:, None, :])
    ratio = tgt_dist[:, None, :] / src_dist[:, :, None]
    p_prev = jnp.ones_like(cosine)
    p_now = cosine
    power = ratio
    total = 1.0 + ratio * cosine
    for level in range(1, ORDER):
        p_next = ((2 * level + 1) * cosine * p_now - level * p_prev) / (level + 1)
        power = power * ratio
        total = total + power * p_next
        p_prev, p_now = (p_now, p_next)
    kernel = total / src_dist[:, :, None]
    return lax.optimization_barrier(jnp.sum(sources[:, 3, :, None] * kernel, axis=1))

def reference(panel_nodes, density, crevice_routes, crevice_centre, centres, targets, centre_home, upsample, fine_weights):
    coarse_all = jnp.concatenate([panel_nodes.reshape(3, PANELS, NODES).transpose(1, 0, 2), density.reshape(PANELS, 1, NODES)], axis=1)
    target_all = targets.reshape(3, CENTRES, NODES)
    pairs = PANELS * TOP
    block = math.gcd(pairs, 4096)
    panel_of = (jnp.arange(pairs, dtype=jnp.int32) // TOP).astype(jnp.int32)
    centre_of = (crevice_routes.reshape(-1) * C_DEV + crevice_centre.reshape(-1)).astype(jnp.int32)

    def one_block(indices):
        panel_ids, centre_ids = indices
        sources = refine(coarse_all[panel_ids], upsample, fine_weights)
        centre_pos = centres[:, centre_ids].T
        target_pos = target_all[:, centre_ids, :].transpose(1, 0, 2)
        return expansion_terms(sources, centre_pos, target_pos)
    terms = lax.map(one_block, (panel_of.reshape(-1, block), centre_of.reshape(-1, block)))
    potential = jax.ops.segment_sum(terms.reshape(pairs, NODES), centre_of, num_segments=CENTRES)
    home = centre_home.reshape(DEVICES, C_DEV)
    rank = jax.vmap(lambda row: route_rank(row, DEVICES))(home)
    owner = jnp.arange(DEVICES, dtype=jnp.int32)[:, None]
    flat_index = ((home * DEVICES + owner) * MOST_BACK + rank).astype(jnp.int32)
    returned = jnp.zeros((DEVICES * DEVICES * MOST_BACK, NODES), jnp.float32).at[flat_index.reshape(-1)].set(potential)
    return returned.reshape(-1)
```

```python
import jax
import jax.numpy as jnp
from jax import lax
from jax.sharding import PartitionSpec as P

ORDER = 8
HI = lax.Precision.HIGHEST


def route_rank(destination, count):
    rows = destination.shape[0]
    onehot = (destination[:, None] == jnp.arange(count, dtype=jnp.int32)[None, :]).astype(jnp.bfloat16)
    lower = (jnp.arange(rows)[:, None] > jnp.arange(rows)[None, :]).astype(jnp.bfloat16)
    before = jnp.dot(lower, onehot, preferred_element_type=jnp.float32)
    return jnp.sum(before * onehot.astype(jnp.float32), axis=1).astype(jnp.int32)


def expansion_terms(fine, strength, centre_pos, rel_targets):
    src = fine - centre_pos[:, None, :]
    rs2 = jnp.sum(src * src, axis=0)
    rt2 = jnp.sum(rel_targets * rel_targets, axis=0)
    inv_rs2 = 1.0 / rs2
    scale = strength * lax.rsqrt(rs2)
    inner = jnp.sum(src[:, :, None, :] * rel_targets[:, None, :, :], axis=0)
    w = inner * inv_rs2[:, None, :]
    rho2 = rt2[None, :, :] * inv_rs2[:, None, :]
    p_prev = jnp.ones_like(w)
    p_now = w
    total = 1.0 + w
    for level in range(1, ORDER):
        p_next = ((2 * level + 1) / (level + 1)) * w * p_now - (level / (level + 1)) * rho2 * p_prev
        total = total + p_next
        p_prev, p_now = (p_now, p_next)
    return jnp.sum(scale[:, None, :] * total, axis=0)


def per_device(
    panel_nodes,
    density,
    crevice_routes,
    crevice_centre,
    centres,
    targets,
    centre_home,
    upsample,
    fine_weights,
):
    devices = lax.axis_size(("grp", "dev"))
    panels = crevice_routes.shape[0]
    fanout = crevice_routes.shape[1]
    centre_count = centres.shape[1]
    capacity = max(2, 2 * panels * fanout // devices)
    capacity_back = max(2, 2 * centre_count // devices)
    fine_count, nodes = upsample.shape
    pairs = panels * fanout
    slots = devices * capacity

    coarse = jnp.concatenate(
        [panel_nodes.reshape(3, panels, nodes).transpose(0, 2, 1).reshape(3 * nodes, panels),
         density.reshape(panels, nodes).T],
        axis=0,
    )
    coarse_pairs = jnp.repeat(coarse, fanout, axis=1)
    ids_pairs = (crevice_centre.reshape(1, pairs) + 1).astype(jnp.float32)
    payload = jnp.concatenate([coarse_pairs, ids_pairs], axis=0)

    destination = crevice_routes.reshape(-1)
    slot_index = destination * capacity + route_rank(destination, devices)
    place = (slot_index[:, None] == jnp.arange(slots, dtype=jnp.int32)[None, :]).astype(jnp.float32)
    outgoing = jnp.dot(payload, place, precision=HI)

    incoming = lax.all_to_all(outgoing, ("grp", "dev"), split_axis=1, concat_axis=1, tiled=True)

    ids = jnp.round(incoming[4 * nodes]).astype(jnp.int32) - 1
    valid = ids >= 0
    pick = (ids[:, None] == jnp.arange(centre_count, dtype=jnp.int32)[None, :]).astype(jnp.float32)

    centre_pos = centres
    rel = targets.reshape(3, centre_count, nodes) - centre_pos[:, :, None]
    centre_data = jnp.concatenate([centre_pos, rel.transpose(0, 2, 1).reshape(3 * nodes, centre_count)], axis=0)
    gathered = lax.dot_general(centre_data, pick, (((1,), (1,)), ((), ())), precision=HI)
    slot_centre = gathered[:3]
    slot_targets = gathered[3:].reshape(3, nodes, slots)

    coarse_in = incoming[: 4 * nodes].reshape(4, nodes, slots)
    upper = jnp.einsum("jn,cns->cjs", upsample, coarse_in, precision=HI)
    strength = upper[3] * fine_weights[:, None]
    terms = expansion_terms(upper[:3], strength, slot_centre, slot_targets)
    terms = jnp.where(valid[None, :], terms, 0.0)

    potential = jnp.dot(terms, pick, precision=HI)

    home = centre_home.reshape(-1)
    back_index = home * capacity_back + route_rank(home, devices)
    back_place = (
        back_index[None, :] == jnp.arange(devices * capacity_back, dtype=jnp.int32)[:, None]
    ).astype(jnp.float32)
    sending = lax.dot_general(back_place, potential, (((1,), (1,)), ((), ())), precision=HI)
    sending = sending.reshape(devices, capacity_back * nodes)
    returned = lax.all_to_all(sending, ("grp", "dev"), split_axis=0, concat_axis=0, tiled=True)
    return returned.reshape(-1)


def solution(mesh):
    placed = (
        P(None, ("grp", "dev")),
        P(("grp", "dev")),
        P(("grp", "dev"), None),
        P(("grp", "dev"), None),
        P(None, ("grp", "dev")),
        P(None, ("grp", "dev")),
        P(("grp", "dev"), None),
        P(),
        P(),
    )
    return jax.shard_map(
        per_device, mesh=mesh, in_specs=placed, out_specs=P(("grp", "dev")), check_vma=False
    )
```

```python
import jax
import jax.numpy as jnp
from jax import lax
from jax.sharding import PartitionSpec as P

ORDER = 8
HI = lax.Precision.HIGHEST
BF = jnp.bfloat16
F32 = jnp.float32


def route_rank(destination, count):
    rows = destination.shape[0]
    onehot = (destination[:, None] == jnp.arange(count, dtype=jnp.int32)[None, :]).astype(BF)
    lower = (jnp.arange(rows)[:, None] > jnp.arange(rows)[None, :]).astype(BF)
    before = jnp.dot(lower, onehot, preferred_element_type=F32)
    return jnp.sum(before * onehot.astype(F32), axis=1).astype(jnp.int32)


def split3(x, axis):
    hi = lax.reduce_precision(x, exponent_bits=8, mantissa_bits=7)
    rest = x - hi
    mid = lax.reduce_precision(rest, exponent_bits=8, mantissa_bits=7)
    lo = rest - mid
    return jnp.concatenate([hi, mid, lo], axis=axis).astype(BF)


def join3(y, axis):
    a, b, c = jnp.split(y, 3, axis=axis)
    return (a + b) + c


def expansion_terms(fine, strength, centre_pos, rel_targets):
    ax = fine[0] - centre_pos[0][None, :]
    ay = fine[1] - centre_pos[1][None, :]
    az = fine[2] - centre_pos[2][None, :]
    bx, by, bz = rel_targets[0], rel_targets[1], rel_targets[2]
    rs2 = ax * ax + ay * ay + az * az
    rt2 = bx * bx + by * by + bz * bz
    inv_rs2 = 1.0 / rs2
    scale = strength * lax.rsqrt(rs2)
    ax = ax * inv_rs2
    ay = ay * inv_rs2
    az = az * inv_rs2
    w = ax[:, None, :] * bx[None] + ay[:, None, :] * by[None] + az[:, None, :] * bz[None]
    rho2 = rt2[None, :, :] * inv_rs2[:, None, :]
    p_prev = jnp.ones_like(w)
    p_now = w
    total = 1.0 + w
    for level in range(1, ORDER):
        p_next = ((2 * level + 1) / (level + 1)) * w * p_now - (level / (level + 1)) * rho2 * p_prev
        total = total + p_next
        p_prev, p_now = (p_now, p_next)
    return jnp.sum(scale[:, None, :] * total, axis=0)


def per_device(
    panel_nodes,
    density,
    crevice_routes,
    crevice_centre,
    centres,
    targets,
    centre_home,
    upsample,
    fine_weights,
):
    devices = lax.axis_size(("grp", "dev"))
    panels = crevice_routes.shape[0]
    fanout = crevice_routes.shape[1]
    centre_count = centres.shape[1]
    capacity = max(2, 2 * panels * fanout // devices)
    capacity_back = max(2, 2 * centre_count // devices)
    fine_count, nodes = upsample.shape
    pairs = panels * fanout
    slots = devices * capacity
    width = 4 * nodes

    coarse = jnp.concatenate(
        [panel_nodes.reshape(3, panels, nodes).transpose(1, 0, 2).reshape(panels, 3 * nodes),
         density.reshape(panels, nodes)],
        axis=1,
    )
    coarse_pairs = jnp.broadcast_to(coarse[:, None, :], (panels, fanout, width)).reshape(pairs, width)
    ids1 = crevice_centre.reshape(pairs) + 1
    id_parts = jnp.stack([ids1 // 16, ids1 % 16], axis=1).astype(BF)
    rhs = jnp.concatenate([split3(coarse_pairs, 1), id_parts], axis=1)

    destination = crevice_routes.reshape(-1)
    slot_index = destination * capacity + route_rank(destination, devices)
    place = (jnp.arange(slots, dtype=jnp.int32)[:, None] == slot_index[None, :]).astype(BF)
    placed = jnp.dot(place, rhs, preferred_element_type=F32)
    payload = join3(placed[:, : 3 * width], 1)
    slot_ids = 16.0 * placed[:, 3 * width] + placed[:, 3 * width + 1]
    outgoing = jnp.concatenate(
        [payload.reshape(devices, capacity * width), slot_ids.reshape(devices, capacity)], axis=1
    )

    incoming = lax.all_to_all(outgoing, ("grp", "dev"), split_axis=0, concat_axis=0, tiled=True)

    coarse_in = incoming[:, : capacity * width].reshape(slots, width)
    ids = jnp.round(incoming[:, capacity * width :]).astype(jnp.int32).reshape(slots) - 1
    valid = ids >= 0
    pick = (jnp.arange(centre_count, dtype=jnp.int32)[:, None] == ids[None, :]).astype(BF)

    rel = targets.reshape(3, centre_count, nodes) - centres[:, :, None]
    centre_data = jnp.concatenate(
        [centres, rel.transpose(0, 2, 1).reshape(3 * nodes, centre_count)], axis=0
    )
    gathered = join3(jnp.dot(split3(centre_data, 0), pick, preferred_element_type=F32), 0)
    slot_centre = gathered[:3]
    slot_targets = gathered[3:].reshape(3, nodes, slots)

    upper = jnp.einsum(
        "jn,scn->cjs", upsample, coarse_in.reshape(slots, 4, nodes), precision=HI
    )
    strength = upper[3] * fine_weights[:, None]
    terms = expansion_terms(upper[:3], strength, slot_centre, slot_targets)
    terms = jnp.where(valid[None, :], terms, 0.0)

    potential = join3(
        lax.dot_general(split3(terms, 0), pick, (((1,), (1,)), ((), ())), preferred_element_type=F32), 0
    )

    home = centre_home.reshape(-1)
    back_index = home * capacity_back + route_rank(home, devices)
    back_place = (
        jnp.arange(devices * capacity_back, dtype=jnp.int32)[:, None] == back_index[None, :]
    ).astype(BF)
    sending = join3(
        lax.dot_general(back_place, split3(potential, 0), (((1,), (1,)), ((), ())), preferred_element_type=F32), 1
    )
    sending = sending.reshape(devices, capacity_back * nodes)
    returned = lax.all_to_all(sending, ("grp", "dev"), split_axis=0, concat_axis=0, tiled=True)
    return returned.reshape(-1)


def solution(mesh):
    placed = (
        P(None, ("grp", "dev")),
        P(("grp", "dev")),
        P(("grp", "dev"), None),
        P(("grp", "dev"), None),
        P(None, ("grp", "dev")),
        P(None, ("grp", "dev")),
        P(("grp", "dev"), None),
        P(),
        P(),
    )
    return jax.shard_map(
        per_device, mesh=mesh, in_specs=placed, out_specs=P(("grp", "dev")), check_vma=False
    )
```

```python
import jax
import jax.numpy as jnp
from jax import lax
from jax.sharding import PartitionSpec as P

ORDER = 8
HI = lax.Precision.HIGHEST
BF = jnp.bfloat16
F32 = jnp.float32


def route_rank(destination, count):
    rows = destination.shape[0]
    onehot = (destination[:, None] == jnp.arange(count, dtype=jnp.int32)[None, :]).astype(BF)
    lower = (jnp.arange(rows)[:, None] > jnp.arange(rows)[None, :]).astype(BF)
    before = jnp.dot(lower, onehot, preferred_element_type=F32)
    return jnp.sum(before * onehot.astype(F32), axis=1).astype(jnp.int32)


def split3(x, axis):
    hi = lax.reduce_precision(x, exponent_bits=8, mantissa_bits=7)
    rest = x - hi
    mid = lax.reduce_precision(rest, exponent_bits=8, mantissa_bits=7)
    lo = rest - mid
    return jnp.concatenate([hi, mid, lo], axis=axis).astype(BF)


def join3(y, axis):
    a, b, c = jnp.split(y, 3, axis=axis)
    return (a + b) + c


def expansion_terms(fine, strength, centre_pos, rel_targets):
    ax = fine[0] - centre_pos[0][None]
    ay = fine[1] - centre_pos[1][None]
    az = fine[2] - centre_pos[2][None]
    bx, by, bz = rel_targets[0], rel_targets[1], rel_targets[2]
    rs2 = ax * ax + ay * ay + az * az
    rt2 = bx * bx + by * by + bz * bz
    inv_rs2 = 1.0 / rs2
    scale = strength * lax.rsqrt(rs2)
    ax = ax * inv_rs2
    ay = ay * inv_rs2
    az = az * inv_rs2
    w = ax[:, None] * bx[None] + ay[:, None] * by[None] + az[:, None] * bz[None]
    rho2 = rt2[None] * inv_rs2[:, None]
    p_prev = jnp.ones_like(w)
    p_now = w
    total = 1.0 + w
    for level in range(1, ORDER):
        p_next = ((2 * level + 1) / (level + 1)) * w * p_now - (level / (level + 1)) * rho2 * p_prev
        total = total + p_next
        p_prev, p_now = (p_now, p_next)
    return jnp.sum(scale[:, None] * total, axis=0)


def per_device(
    panel_nodes,
    density,
    crevice_routes,
    crevice_centre,
    centres,
    targets,
    centre_home,
    upsample,
    fine_weights,
):
    devices = lax.axis_size(("grp", "dev"))
    panels = crevice_routes.shape[0]
    fanout = crevice_routes.shape[1]
    centre_count = centres.shape[1]
    capacity = max(2, 2 * panels * fanout // devices)
    capacity_back = max(2, 2 * centre_count // devices)
    fine_count, nodes = upsample.shape
    pairs = panels * fanout
    slots = devices * capacity
    width = 4 * nodes

    coarse = jnp.concatenate(
        [panel_nodes.reshape(3, panels, nodes).transpose(1, 0, 2).reshape(panels, 3 * nodes),
         density.reshape(panels, nodes)],
        axis=1,
    )
    coarse_pairs = jnp.broadcast_to(coarse[:, None, :], (panels, fanout, width)).reshape(pairs, width)
    ids1 = crevice_centre.reshape(pairs) + 1
    id_parts = jnp.stack([ids1 // 16, ids1 % 16], axis=1).astype(BF)
    rhs = jnp.concatenate([split3(coarse_pairs, 1), id_parts], axis=1)

    destination = crevice_routes.reshape(-1)
    slot_index = destination * capacity + route_rank(destination, devices)
    place = (jnp.arange(slots, dtype=jnp.int32)[:, None] == slot_index[None, :]).astype(BF)
    placed = jnp.dot(place, rhs, preferred_element_type=F32)
    payload = join3(placed[:, : 3 * width], 1)
    slot_ids = 16.0 * placed[:, 3 * width] + placed[:, 3 * width + 1]
    outgoing = jnp.concatenate(
        [payload.reshape(devices, capacity * width), slot_ids.reshape(devices, capacity)], axis=1
    )

    incoming = lax.all_to_all(outgoing, ("grp", "dev"), split_axis=0, concat_axis=0, tiled=True)

    coarse_in = incoming[:, : capacity * width].reshape(slots // 2, 2 * width)
    ids = jnp.round(incoming[:, capacity * width :]).astype(jnp.int32)
    ids = ids.reshape(devices, capacity // 2, 2).transpose(2, 0, 1).reshape(slots) - 1
    valid = ids >= 0
    pick = (jnp.arange(centre_count, dtype=jnp.int32)[:, None] == ids[None, :]).astype(BF)

    rel = targets.reshape(3, centre_count, nodes) - centres[:, :, None]
    centre_data = jnp.concatenate(
        [centres, rel.transpose(0, 2, 1).reshape(3 * nodes, centre_count)], axis=0
    )
    gathered = join3(jnp.dot(split3(centre_data, 0), pick, preferred_element_type=F32), 0)
    slot_centre = gathered[:3].reshape(3, 2, slots // 2)
    slot_targets = gathered[3:].reshape(3, nodes, 2, slots // 2)

    eye_c = jnp.eye(4, dtype=F32)
    eye_p = jnp.eye(2, dtype=F32)
    refine_w = (
        eye_c[:, None, None, None, :, None] * upsample[None, :, None, None, None, :] * eye_p[None, None, :, :, None, None]
    ).reshape(4 * fine_count * 2, 2 * width)
    upper = lax.dot_general(refine_w, coarse_in, (((1,), (1,)), ((), ())), precision=HI)
    upper = upper.reshape(4, fine_count, 2, slots // 2)
    strength = upper[3] * fine_weights[:, None, None]
    terms = expansion_terms(upper[:3], strength, slot_centre, slot_targets).reshape(nodes, slots)
    terms = jnp.where(valid[None, :], terms, 0.0)

    potential = join3(
        lax.dot_general(split3(terms, 0), pick, (((1,), (1,)), ((), ())), preferred_element_type=F32), 0
    )

    home = centre_home.reshape(-1)
    back_index = home * capacity_back + route_rank(home, devices)
    back_place = (
        jnp.arange(devices * capacity_back, dtype=jnp.int32)[:, None] == back_index[None, :]
    ).astype(BF)
    sending = join3(
        lax.dot_general(back_place, split3(potential, 0), (((1,), (1,)), ((), ())), preferred_element_type=F32), 1
    )
    sending = sending.reshape(devices, capacity_back * nodes)
    returned = lax.all_to_all(sending, ("grp", "dev"), split_axis=0, concat_axis=0, tiled=True)
    return returned.reshape(-1)


def solution(mesh):
    placed = (
        P(None, ("grp", "dev")),
        P(("grp", "dev")),
        P(("grp", "dev"), None),
        P(("grp", "dev"), None),
        P(None, ("grp", "dev")),
        P(None, ("grp", "dev")),
        P(("grp", "dev"), None),
        P(),
        P(),
    )
    return jax.shard_map(
        per_device, mesh=mesh, in_specs=placed, out_specs=P(("grp", "dev")), check_vma=False
    )
```

```python
import jax
import jax.numpy as jnp
from jax import lax
from jax.sharding import PartitionSpec as P

ORDER = 8
HI = lax.Precision.HIGHEST
BF = jnp.bfloat16
F32 = jnp.float32


def route_rank(destination, count):
    rows = destination.shape[0]
    onehot = (destination[:, None] == jnp.arange(count, dtype=jnp.int32)[None, :]).astype(BF)
    lower = (jnp.arange(rows)[:, None] > jnp.arange(rows)[None, :]).astype(BF)
    before = jnp.dot(lower, onehot, preferred_element_type=F32)
    return jnp.sum(before * onehot.astype(F32), axis=1).astype(jnp.int32)


def split3(x, axis):
    hi = lax.reduce_precision(x, exponent_bits=8, mantissa_bits=7)
    rest = x - hi
    mid = lax.reduce_precision(rest, exponent_bits=8, mantissa_bits=7)
    lo = rest - mid
    return jnp.concatenate([hi, mid, lo], axis=axis).astype(BF)


def join3(y, axis):
    a, b, c = jnp.split(y, 3, axis=axis)
    return (a + b) + c


def clenshaw_constants(order):
    c1 = [(2 * l + 1) / (l + 1) for l in range(order + 1)]
    c2 = [l / (l + 1) for l in range(order + 2)]
    mu = [1.0] * (order + 1)
    for l in range(order - 1, -1, -1):
        mu[l] = c1[l] * mu[l + 1]
    gamma = [c2[l + 1] / (c1[l] * c1[l + 1]) for l in range(order - 1)]
    return mu, gamma


def expansion_terms(fine, strength, centre_pos, rel_targets):
    mu, gamma = clenshaw_constants(ORDER)
    ax = fine[0] - centre_pos[0][None]
    ay = fine[1] - centre_pos[1][None]
    az = fine[2] - centre_pos[2][None]
    bx, by, bz = rel_targets[0], rel_targets[1], rel_targets[2]
    rs2 = ax * ax + ay * ay + az * az
    rt2 = bx * bx + by * by + bz * bz
    inv_rs2 = 1.0 / rs2
    scale = (strength * mu[0]) * lax.rsqrt(rs2)
    ax = ax * inv_rs2
    ay = ay * inv_rs2
    az = az * inv_rs2
    w = ax[:, None] * bx[None] + ay[:, None] * by[None] + az[:, None] * bz[None]
    rho2 = rt2[None] * inv_rs2[:, None]
    t_next = w + (1.0 / mu[ORDER - 1])
    t_after = jnp.ones_like(w)
    for level in range(ORDER - 2, -1, -1):
        t_now = (w * t_next + (1.0 / mu[level])) - gamma[level] * (rho2 * t_after)
        t_after, t_next = (t_next, t_now)
    return jnp.sum(scale[:, None] * t_next, axis=0)


def per_device(
    panel_nodes,
    density,
    crevice_routes,
    crevice_centre,
    centres,
    targets,
    centre_home,
    upsample,
    fine_weights,
):
    devices = lax.axis_size(("grp", "dev"))
    panels = crevice_routes.shape[0]
    fanout = crevice_routes.shape[1]
    centre_count = centres.shape[1]
    capacity = max(2, 2 * panels * fanout // devices)
    capacity_back = max(2, 2 * centre_count // devices)
    fine_count, nodes = upsample.shape
    pairs = panels * fanout
    slots = devices * capacity
    width = 4 * nodes

    coarse = jnp.concatenate(
        [panel_nodes.reshape(3, panels, nodes).transpose(1, 0, 2).reshape(panels, 3 * nodes),
         density.reshape(panels, nodes)],
        axis=1,
    )
    coarse_pairs = jnp.broadcast_to(coarse[:, None, :], (panels, fanout, width)).reshape(pairs, width)
    ids1 = crevice_centre.reshape(pairs) + 1
    id_parts = jnp.stack([ids1 // 16, ids1 % 16], axis=1).astype(BF)
    parts = split3(coarse_pairs, 1).reshape(pairs, 3, 1, width)
    none = jnp.zeros_like(parts)
    none_id = jnp.zeros_like(id_parts)
    rhs = jnp.concatenate(
        [
            jnp.concatenate([jnp.concatenate([parts, none], 2).reshape(pairs, 6 * width), id_parts, none_id], 1),
            jnp.concatenate([jnp.concatenate([none, parts], 2).reshape(pairs, 6 * width), none_id, id_parts], 1),
        ],
        0,
    )

    destination = crevice_routes.reshape(-1)
    slot_index = destination * capacity + route_rank(destination, devices)
    row_slot = 2 * jnp.arange(slots // 2, dtype=jnp.int32)[:, None]
    place = jnp.concatenate(
        [(row_slot == slot_index[None, :]), (row_slot + 1 == slot_index[None, :])], axis=1
    ).astype(BF)
    placed = jnp.dot(place, rhs, preferred_element_type=F32)
    payload = join3(placed[:, : 6 * width], 1)
    slot_ids = 16.0 * placed[:, 6 * width :: 2] + placed[:, 6 * width + 1 :: 2]
    outgoing = jnp.concatenate(
        [payload.reshape(devices, capacity * width), slot_ids.reshape(devices, capacity)], axis=1
    )

    incoming = lax.all_to_all(outgoing, ("grp", "dev"), split_axis=0, concat_axis=0, tiled=True)

    coarse_in = incoming[:, : capacity * width].reshape(slots // 2, 2 * width)
    ids = jnp.round(incoming[:, capacity * width :]).astype(jnp.int32)
    ids = ids.reshape(devices, capacity // 2, 2).transpose(2, 0, 1).reshape(slots) - 1
    valid = ids >= 0
    pick = (jnp.arange(centre_count, dtype=jnp.int32)[:, None] == ids[None, :]).astype(BF)

    rel = targets.reshape(3, centre_count, nodes) - centres[:, :, None]
    centre_data = jnp.concatenate(
        [centres, rel.transpose(0, 2, 1).reshape(3 * nodes, centre_count)], axis=0
    )
    gathered = join3(jnp.dot(split3(centre_data, 0), pick, preferred_element_type=F32), 0)
    slot_centre = gathered[:3].reshape(3, 2, slots // 2)
    slot_targets = gathered[3:].reshape(3, nodes, 2, slots // 2)

    eye_c = jnp.eye(4, dtype=F32)
    eye_p = jnp.eye(2, dtype=F32)
    refine_w = (
        eye_c[:, None, None, None, :, None] * upsample[None, :, None, None, None, :] * eye_p[None, None, :, :, None, None]
    ).reshape(4 * fine_count * 2, 2 * width)
    upper = lax.dot_general(refine_w, coarse_in, (((1,), (1,)), ((), ())), precision=HI)
    upper = upper.reshape(4, fine_count, 2, slots // 2)
    strength = upper[3] * fine_weights[:, None, None]
    terms = expansion_terms(upper[:3], strength, slot_centre, slot_targets).reshape(nodes, slots)
    terms = jnp.where(valid[None, :], terms, 0.0)

    potential = join3(
        lax.dot_general(split3(terms, 0), pick, (((1,), (1,)), ((), ())), preferred_element_type=F32), 0
    )

    home = centre_home.reshape(-1)
    back_index = home * capacity_back + route_rank(home, devices)
    back_place = (
        jnp.arange(devices * capacity_back, dtype=jnp.int32)[:, None] == back_index[None, :]
    ).astype(BF)
    sending = join3(
        lax.dot_general(back_place, split3(potential, 0), (((1,), (1,)), ((), ())), preferred_element_type=F32), 1
    )
    sending = sending.reshape(devices, capacity_back * nodes)
    returned = lax.all_to_all(sending, ("grp", "dev"), split_axis=0, concat_axis=0, tiled=True)
    return returned.reshape(-1)


def solution(mesh):
    placed = (
        P(None, ("grp", "dev")),
        P(("grp", "dev")),
        P(("grp", "dev"), None),
        P(("grp", "dev"), None),
        P(None, ("grp", "dev")),
        P(None, ("grp", "dev")),
        P(("grp", "dev"), None),
        P(),
        P(),
    )
    return jax.shard_map(
        per_device, mesh=mesh, in_specs=placed, out_specs=P(("grp", "dev")), check_vma=False
    )
```

```python
import jax
import jax.numpy as jnp
from jax import lax
from jax.sharding import PartitionSpec as P

ORDER = 8
HI = lax.Precision.HIGHEST
BF = jnp.bfloat16
F32 = jnp.float32


def route_rank(destination, count):
    rows = destination.shape[0]
    onehot = (destination[:, None] == jnp.arange(count, dtype=jnp.int32)[None, :]).astype(BF)
    lower = (jnp.arange(rows)[:, None] > jnp.arange(rows)[None, :]).astype(BF)
    before = jnp.dot(lower, onehot, preferred_element_type=F32)
    return jnp.sum(before * onehot.astype(F32), axis=1).astype(jnp.int32)


def split3(x, axis):
    hi = lax.reduce_precision(x, exponent_bits=8, mantissa_bits=7)
    rest = x - hi
    mid = lax.reduce_precision(rest, exponent_bits=8, mantissa_bits=7)
    lo = rest - mid
    return jnp.concatenate([hi, mid, lo], axis=axis).astype(BF)


def join3(y, axis):
    a, b, c = jnp.split(y, 3, axis=axis)
    return (a + b) + c


def clenshaw_constants(order):
    c1 = [(2 * l + 1) / (l + 1) for l in range(order + 1)]
    c2 = [l / (l + 1) for l in range(order + 2)]
    mu = [1.0] * (order + 1)
    for l in range(order - 1, -1, -1):
        mu[l] = c1[l] * mu[l + 1]
    gamma = [c2[l + 1] / (c1[l] * c1[l + 1]) for l in range(order - 1)]
    return mu, gamma


def expansion_terms(fine, strength, centre_pos, rel_targets):
    mu, gamma = clenshaw_constants(ORDER)
    ax = fine[0] - centre_pos[0][None]
    ay = fine[1] - centre_pos[1][None]
    az = fine[2] - centre_pos[2][None]
    bx, by, bz = rel_targets[0], rel_targets[1], rel_targets[2]
    rs2 = ax * ax + ay * ay + az * az
    rt2 = bx * bx + by * by + bz * bz
    inv_rs2 = 1.0 / rs2
    scale = (strength * mu[0]) * lax.rsqrt(rs2)
    ax = ax * inv_rs2
    ay = ay * inv_rs2
    az = az * inv_rs2
    w = ax[:, None] * bx[None] + ay[:, None] * by[None] + az[:, None] * bz[None]
    rho2 = rt2[None] * inv_rs2[:, None]
    t_next = w + (1.0 / mu[ORDER - 1])
    t_after = jnp.ones_like(w)
    for level in range(ORDER - 2, -1, -1):
        t_now = (w * t_next + (1.0 / mu[level])) - gamma[level] * (rho2 * t_after)
        t_after, t_next = (t_next, t_now)
    return jnp.sum(scale[:, None] * t_next, axis=0)


def per_device(
    panel_nodes,
    density,
    crevice_routes,
    crevice_centre,
    centres,
    targets,
    centre_home,
    upsample,
    fine_weights,
):
    devices = lax.axis_size(("grp", "dev"))
    panels = crevice_routes.shape[0]
    fanout = crevice_routes.shape[1]
    centre_count = centres.shape[1]
    capacity = max(2, 2 * panels * fanout // devices)
    capacity_back = max(2, 2 * centre_count // devices)
    fine_count, nodes = upsample.shape
    pairs = panels * fanout
    slots = devices * capacity
    width = 4 * nodes

    coarse = jnp.concatenate(
        [panel_nodes.reshape(3, panels, nodes).transpose(1, 0, 2).reshape(panels, 3 * nodes),
         density.reshape(panels, nodes)],
        axis=1,
    )
    coarse_pairs = jnp.broadcast_to(coarse[:, None, :], (panels, fanout, width)).reshape(pairs, width)
    ids1 = crevice_centre.reshape(pairs) + 1
    id_parts = jnp.stack([ids1 // 16, ids1 % 16], axis=1).astype(BF)
    rhs = jnp.concatenate([split3(coarse_pairs, 1), id_parts], axis=1)

    destination = crevice_routes.reshape(-1)
    slot_index = destination * capacity + route_rank(destination, devices)
    place = (jnp.arange(slots, dtype=jnp.int32)[:, None] == slot_index[None, :]).astype(BF)
    placed = jnp.dot(place, rhs, preferred_element_type=F32)
    payload = join3(placed[:, : 3 * width], 1)
    slot_ids = 16.0 * placed[:, 3 * width] + placed[:, 3 * width + 1]
    outgoing = jnp.concatenate(
        [payload.reshape(devices, capacity * width), slot_ids.reshape(devices, capacity)], axis=1
    )

    incoming = lax.all_to_all(outgoing, ("grp", "dev"), split_axis=0, concat_axis=0, tiled=True)

    coarse_in = incoming[:, : capacity * width].reshape(slots // 2, 2 * width)
    ids = jnp.round(incoming[:, capacity * width :]).astype(jnp.int32)
    ids = ids.reshape(devices, capacity // 2, 2).transpose(2, 0, 1).reshape(slots) - 1
    valid = ids >= 0
    pick = (jnp.arange(centre_count, dtype=jnp.int32)[:, None] == ids[None, :]).astype(BF)

    rel = targets.reshape(3, centre_count, nodes) - centres[:, :, None]
    centre_data = jnp.concatenate(
        [centres, rel.transpose(0, 2, 1).reshape(3 * nodes, centre_count)], axis=0
    )
    gathered = join3(jnp.dot(split3(centre_data, 0), pick, preferred_element_type=F32), 0)
    slot_centre = gathered[:3].reshape(3, 2, slots // 2)
    slot_targets = gathered[3:].reshape(3, nodes, 2, slots // 2)

    eye_c = jnp.eye(4, dtype=F32)
    eye_p = jnp.eye(2, dtype=F32)
    refine_w = (
        eye_c[:, None, None, None, :, None] * upsample[None, :, None, None, None, :] * eye_p[None, None, :, :, None, None]
    ).reshape(4 * fine_count * 2, 2 * width)
    upper = lax.dot_general(refine_w, coarse_in, (((1,), (1,)), ((), ())), precision=HI)
    upper = upper.reshape(4, fine_count, 2, slots // 2)
    strength = upper[3] * fine_weights[:, None, None]
    terms = expansion_terms(upper[:3], strength, slot_centre, slot_targets).reshape(nodes, slots)
    terms = jnp.where(valid[None, :], terms, 0.0)

    potential = join3(
        lax.dot_general(split3(terms, 0), pick, (((1,), (1,)), ((), ())), preferred_element_type=F32), 0
    )

    home = centre_home.reshape(-1)
    back_index = home * capacity_back + route_rank(home, devices)
    back_place = (
        jnp.arange(devices * capacity_back, dtype=jnp.int32)[:, None] == back_index[None, :]
    ).astype(BF)
    sending = join3(
        lax.dot_general(back_place, split3(potential, 0), (((1,), (1,)), ((), ())), preferred_element_type=F32), 1
    )
    sending = sending.reshape(devices, capacity_back * nodes)
    returned = lax.all_to_all(sending, ("grp", "dev"), split_axis=0, concat_axis=0, tiled=True)
    return returned.reshape(-1)


def solution(mesh):
    placed = (
        P(None, ("grp", "dev")),
        P(("grp", "dev")),
        P(("grp", "dev"), None),
        P(("grp", "dev"), None),
        P(None, ("grp", "dev")),
        P(None, ("grp", "dev")),
        P(("grp", "dev"), None),
        P(),
        P(),
    )
    return jax.shard_map(
        per_device, mesh=mesh, in_specs=placed, out_specs=P(("grp", "dev")), check_vma=False
    )
```

```python
import jax
import jax.numpy as jnp
from jax import lax
from jax.sharding import PartitionSpec as P

ORDER = 8
HI = lax.Precision.HIGHEST
BF = jnp.bfloat16
F32 = jnp.float32


def route_rank(destination, count):
    rows = destination.shape[0]
    onehot = (destination[:, None] == jnp.arange(count, dtype=jnp.int32)[None, :]).astype(BF)
    lower = (jnp.arange(rows)[:, None] > jnp.arange(rows)[None, :]).astype(BF)
    before = jnp.dot(lower, onehot, preferred_element_type=F32)
    return jnp.sum(before * onehot.astype(F32), axis=1).astype(jnp.int32)


def split3(x, axis):
    hi = lax.reduce_precision(x, exponent_bits=8, mantissa_bits=7)
    rest = x - hi
    mid = lax.reduce_precision(rest, exponent_bits=8, mantissa_bits=7)
    lo = rest - mid
    return jnp.concatenate([hi, mid, lo], axis=axis).astype(BF)


def join3(y, axis):
    a, b, c = jnp.split(y, 3, axis=axis)
    return (a + b) + c


def clenshaw_constants(order):
    c1 = [(2 * l + 1) / (l + 1) for l in range(order + 1)]
    c2 = [l / (l + 1) for l in range(order + 2)]
    mu = [1.0] * (order + 1)
    for l in range(order - 1, -1, -1):
        mu[l] = c1[l] * mu[l + 1]
    gamma = [c2[l + 1] / (c1[l] * c1[l + 1]) for l in range(order - 1)]
    return mu, gamma


def expansion_terms(fine, strength, centre_pos, rel_targets):
    mu, gamma = clenshaw_constants(ORDER)
    ax = fine[:, 0] - centre_pos[:, 0][:, None]
    ay = fine[:, 1] - centre_pos[:, 1][:, None]
    az = fine[:, 2] - centre_pos[:, 2][:, None]
    bx, by, bz = rel_targets[:, 0], rel_targets[:, 1], rel_targets[:, 2]
    rs2 = ax * ax + ay * ay + az * az
    rt2 = bx * bx + by * by + bz * bz
    inv_rs2 = 1.0 / rs2
    scale = (strength * mu[0]) * lax.rsqrt(rs2)
    ax = ax * inv_rs2
    ay = ay * inv_rs2
    az = az * inv_rs2
    w = ax[:, :, None] * bx[:, None] + ay[:, :, None] * by[:, None] + az[:, :, None] * bz[:, None]
    rho2 = rt2[:, None] * inv_rs2[:, :, None]
    t_next = w + (1.0 / mu[ORDER - 1])
    t_after = jnp.ones_like(w)
    for level in range(ORDER - 2, -1, -1):
        t_now = (w * t_next + (1.0 / mu[level])) - gamma[level] * (rho2 * t_after)
        t_after, t_next = (t_next, t_now)
    return jnp.sum(scale[:, :, None] * t_next, axis=1)


def per_device(
    panel_nodes,
    density,
    crevice_routes,
    crevice_centre,
    centres,
    targets,
    centre_home,
    upsample,
    fine_weights,
):
    devices = lax.axis_size(("grp", "dev"))
    panels = crevice_routes.shape[0]
    fanout = crevice_routes.shape[1]
    centre_count = centres.shape[1]
    capacity = max(2, 2 * panels * fanout // devices)
    capacity_back = max(2, 2 * centre_count // devices)
    fine_count, nodes = upsample.shape
    pairs = panels * fanout
    slots = devices * capacity
    width = 4 * nodes

    coarse = jnp.concatenate(
        [panel_nodes.reshape(3, panels, nodes).transpose(1, 0, 2).reshape(panels, 3 * nodes),
         density.reshape(panels, nodes)],
        axis=1,
    )
    coarse_pairs = jnp.broadcast_to(coarse[:, None, :], (panels, fanout, width)).reshape(pairs, width)
    ids1 = crevice_centre.reshape(pairs) + 1
    id_parts = jnp.stack([ids1 // 16, ids1 % 16], axis=1).astype(BF)
    rhs = jnp.concatenate([split3(coarse_pairs, 1), id_parts], axis=1)

    destination = crevice_routes.reshape(-1)
    slot_index = destination * capacity + route_rank(destination, devices)
    place = (jnp.arange(slots, dtype=jnp.int32)[:, None] == slot_index[None, :]).astype(BF)
    placed = jnp.dot(place, rhs, preferred_element_type=F32)
    payload = join3(placed[:, : 3 * width], 1)
    slot_ids = 16.0 * placed[:, 3 * width] + placed[:, 3 * width + 1]
    outgoing = jnp.concatenate(
        [
            payload.reshape(devices, capacity * width),
            slot_ids.reshape(devices, capacity),
            jnp.zeros((devices, 2 * width - capacity), F32),
        ],
        axis=1,
    )

    incoming = lax.all_to_all(outgoing, ("grp", "dev"), split_axis=0, concat_axis=0, tiled=True)

    rows = capacity // 2
    block = incoming.reshape(devices, rows + 1, 2 * width)
    coarse_in = block[:, :rows, :].reshape(slots // 2, 2 * width)
    ids = jnp.round(block[:, rows, :capacity]).astype(jnp.int32)
    ids = ids.reshape(devices, rows, 2).transpose(2, 0, 1).reshape(2, slots // 2) - 1
    valid = ids >= 0
    pick = (jnp.arange(centre_count, dtype=jnp.int32)[None, :, None] == ids[:, None, :]).astype(BF)

    rel = targets.reshape(3, centre_count, nodes) - centres[:, :, None]
    data_rows = 3 + 3 * nodes
    padded_rows = -(-data_rows // 8) * 8
    centre_data = jnp.concatenate(
        [
            centres,
            rel.transpose(0, 2, 1).reshape(3 * nodes, centre_count),
            jnp.zeros((padded_rows - data_rows, centre_count), F32),
        ],
        axis=0,
    )
    gathered = join3(jnp.einsum("fg,pgs->pfs", split3(centre_data, 0), pick, preferred_element_type=F32), 1)
    slot_centre = gathered[:, :3]
    slot_targets = gathered[:, 3:data_rows].reshape(2, 3, nodes, slots // 2)

    eye_c = jnp.eye(4, dtype=F32)
    eye_p = jnp.eye(2, dtype=F32)
    refine_w = (
        eye_p[:, None, None, :, None, None] * eye_c[None, :, None, None, :, None] * upsample[None, None, :, None, None, :]
    ).reshape(2 * 4 * fine_count, 2 * width)
    upper = lax.dot_general(refine_w, coarse_in, (((1,), (1,)), ((), ())), precision=HI)
    upper = upper.reshape(2, 4, fine_count, slots // 2)
    strength = upper[:, 3] * fine_weights[None, :, None]
    terms = expansion_terms(upper[:, :3], strength, slot_centre, slot_targets)
    terms = jnp.where(valid[:, None, :], terms, 0.0)

    potential = join3(jnp.einsum("pks,pgs->kg", split3(terms, 1), pick, preferred_element_type=F32), 0)

    home = centre_home.reshape(-1)
    back_index = home * capacity_back + route_rank(home, devices)
    back_place = (
        jnp.arange(devices * capacity_back, dtype=jnp.int32)[:, None] == back_index[None, :]
    ).astype(BF)
    sending = join3(
        lax.dot_general(back_place, split3(potential, 0), (((1,), (1,)), ((), ())), preferred_element_type=F32), 1
    )
    sending = sending.reshape(devices, capacity_back * nodes)
    returned = lax.all_to_all(sending, ("grp", "dev"), split_axis=0, concat_axis=0, tiled=True)
    return returned.reshape(-1)


def solution(mesh):
    placed = (
        P(None, ("grp", "dev")),
        P(("grp", "dev")),
        P(("grp", "dev"), None),
        P(("grp", "dev"), None),
        P(None, ("grp", "dev")),
        P(None, ("grp", "dev")),
        P(("grp", "dev"), None),
        P(),
        P(),
    )
    return jax.shard_map(
        per_device, mesh=mesh, in_specs=placed, out_specs=P(("grp", "dev")), check_vma=False
    )
```

```python
import jax
import jax.numpy as jnp
from jax import lax
from jax.sharding import PartitionSpec as P

ORDER = 8
HI = lax.Precision.HIGHEST
BF = jnp.bfloat16
F32 = jnp.float32


def route_rank(destination, count):
    rows = destination.shape[0]
    onehot = (destination[:, None] == jnp.arange(count, dtype=jnp.int32)[None, :]).astype(BF)
    lower = (jnp.arange(rows)[:, None] > jnp.arange(rows)[None, :]).astype(BF)
    before = jnp.dot(lower, onehot, preferred_element_type=F32)
    return jnp.sum(before * onehot.astype(F32), axis=1).astype(jnp.int32)


def split3(x, axis):
    hi = lax.reduce_precision(x, exponent_bits=8, mantissa_bits=7)
    rest = x - hi
    mid = lax.reduce_precision(rest, exponent_bits=8, mantissa_bits=7)
    lo = rest - mid
    return jnp.concatenate([hi, mid, lo], axis=axis).astype(BF)


def join3(y, axis):
    a, b, c = jnp.split(y, 3, axis=axis)
    return (a + b) + c


def clenshaw_constants(order):
    c1 = [(2 * l + 1) / (l + 1) for l in range(order + 1)]
    c2 = [l / (l + 1) for l in range(order + 2)]
    mu = [1.0] * (order + 1)
    for l in range(order - 1, -1, -1):
        mu[l] = c1[l] * mu[l + 1]
    gamma = [c2[l + 1] / (c1[l] * c1[l + 1]) for l in range(order - 1)]
    return mu, gamma


def expansion_terms(fine, strength, centre_pos, rel_targets):
    mu, gamma = clenshaw_constants(ORDER)
    ax = fine[:, 0] - centre_pos[:, 0][:, None]
    ay = fine[:, 1] - centre_pos[:, 1][:, None]
    az = fine[:, 2] - centre_pos[:, 2][:, None]
    bx, by, bz = rel_targets[:, 0], rel_targets[:, 1], rel_targets[:, 2]
    rs2 = ax * ax + ay * ay + az * az
    rt2 = bx * bx + by * by + bz * bz
    inv_rs2 = 1.0 / rs2
    scale = (strength * mu[0]) * lax.rsqrt(rs2)
    ax = ax * inv_rs2
    ay = ay * inv_rs2
    az = az * inv_rs2
    w = ax[:, :, None] * bx[:, None] + ay[:, :, None] * by[:, None] + az[:, :, None] * bz[:, None]
    rho2 = rt2[:, None] * inv_rs2[:, :, None]
    t_next = w + (1.0 / mu[ORDER - 1])
    t_after = jnp.ones_like(w)
    for level in range(ORDER - 2, -1, -1):
        t_now = (w * t_next + (1.0 / mu[level])) - gamma[level] * (rho2 * t_after)
        t_after, t_next = (t_next, t_now)
    return jnp.sum(scale[:, :, None] * t_next, axis=1)


def per_device(
    panel_nodes,
    density,
    crevice_routes,
    crevice_centre,
    centres,
    targets,
    centre_home,
    upsample,
    fine_weights,
):
    devices = lax.axis_size(("grp", "dev"))
    panels = crevice_routes.shape[0]
    fanout = crevice_routes.shape[1]
    centre_count = centres.shape[1]
    capacity = max(2, 2 * panels * fanout // devices)
    capacity_back = max(2, 2 * centre_count // devices)
    fine_count, nodes = upsample.shape
    pairs = panels * fanout
    slots = devices * capacity
    width = 4 * nodes

    coarse = jnp.concatenate(
        [panel_nodes.reshape(3, panels, nodes).transpose(1, 0, 2).reshape(panels, 3 * nodes),
         density.reshape(panels, nodes)],
        axis=1,
    )
    coarse_parts = jnp.concatenate([split3(coarse, 1)] * fanout, axis=0)
    ids1 = jnp.concatenate([crevice_centre[:, t] for t in range(fanout)]) + 1
    id_parts = jnp.stack([ids1 // 16, ids1 % 16], axis=1).astype(BF)
    rhs = jnp.concatenate([coarse_parts, id_parts], axis=1)

    destination = jnp.concatenate([crevice_routes[:, t] for t in range(fanout)])
    slot_index = destination * capacity + route_rank(destination, devices)
    place = (jnp.arange(slots, dtype=jnp.int32)[:, None] == slot_index[None, :]).astype(BF)
    placed = jnp.dot(place, rhs, preferred_element_type=F32)
    payload = join3(placed[:, : 3 * width], 1)
    slot_ids = 16.0 * placed[:, 3 * width] + placed[:, 3 * width + 1]
    outgoing = jnp.concatenate(
        [
            payload.reshape(devices, capacity * width),
            slot_ids.reshape(devices, capacity),
            jnp.zeros((devices, 2 * width - capacity), F32),
        ],
        axis=1,
    )

    incoming = lax.all_to_all(outgoing, ("grp", "dev"), split_axis=0, concat_axis=0, tiled=True)

    rows = capacity // 2
    block = incoming.reshape(devices, rows + 1, 2 * width)
    coarse_in = block[:, :rows, :].reshape(slots // 2, 2 * width)
    ids = jnp.round(block[:, rows, :capacity]).astype(jnp.int32)
    ids = ids.reshape(devices, rows, 2).transpose(2, 0, 1).reshape(2, slots // 2) - 1
    valid = ids >= 0
    pick = (jnp.arange(centre_count, dtype=jnp.int32)[None, :, None] == ids[:, None, :]).astype(BF)

    rel = targets.reshape(3, centre_count, nodes) - centres[:, :, None]
    data_rows = 3 + 3 * nodes
    padded_rows = -(-data_rows // 8) * 8
    centre_data = jnp.concatenate(
        [
            centres,
            rel.transpose(0, 2, 1).reshape(3 * nodes, centre_count),
            jnp.zeros((padded_rows - data_rows, centre_count), F32),
        ],
        axis=0,
    )
    gathered = join3(jnp.einsum("fg,pgs->pfs", split3(centre_data, 0), pick, preferred_element_type=F32), 1)
    slot_centre = gathered[:, :3]
    slot_targets = gathered[:, 3:data_rows].reshape(2, 3, nodes, slots // 2)

    eye_c = jnp.eye(4, dtype=F32)
    eye_p = jnp.eye(2, dtype=F32)
    refine_w = (
        eye_p[:, None, None, :, None, None] * eye_c[None, :, None, None, :, None] * upsample[None, None, :, None, None, :]
    ).reshape(2 * 4 * fine_count, 2 * width)
    upper = lax.dot_general(refine_w, coarse_in, (((1,), (1,)), ((), ())), precision=HI)
    upper = upper.reshape(2, 4, fine_count, slots // 2)
    strength = upper[:, 3] * fine_weights[None, :, None]
    terms = expansion_terms(upper[:, :3], strength, slot_centre, slot_targets)
    terms = jnp.where(valid[:, None, :], terms, 0.0)

    potential = join3(jnp.einsum("pks,pgs->kg", split3(terms, 1), pick, preferred_element_type=F32), 0)

    home = centre_home.reshape(-1)
    back_index = home * capacity_back + route_rank(home, devices)
    back_place = (
        jnp.arange(devices * capacity_back, dtype=jnp.int32)[:, None] == back_index[None, :]
    ).astype(BF)
    sending = join3(
        lax.dot_general(back_place, split3(potential, 0), (((1,), (1,)), ((), ())), preferred_element_type=F32), 1
    )
    sending = sending.reshape(devices, capacity_back * nodes)
    returned = lax.all_to_all(sending, ("grp", "dev"), split_axis=0, concat_axis=0, tiled=True)
    return returned.reshape(-1)


def solution(mesh):
    placed = (
        P(None, ("grp", "dev")),
        P(("grp", "dev")),
        P(("grp", "dev"), None),
        P(("grp", "dev"), None),
        P(None, ("grp", "dev")),
        P(None, ("grp", "dev")),
        P(("grp", "dev"), None),
        P(),
        P(),
    )
    return jax.shard_map(
        per_device, mesh=mesh, in_specs=placed, out_specs=P(("grp", "dev")), check_vma=False
    )
```

```python
import jax
import jax.numpy as jnp
from jax import lax
from jax.sharding import PartitionSpec as P

ORDER = 8
HI = lax.Precision.HIGHEST
BF = jnp.bfloat16
F32 = jnp.float32


def route_rank(destination, count):
    rows = destination.shape[0]
    onehot = (destination[:, None] == jnp.arange(count, dtype=jnp.int32)[None, :]).astype(BF)
    lower = (jnp.arange(rows)[:, None] > jnp.arange(rows)[None, :]).astype(BF)
    before = jnp.dot(lower, onehot, preferred_element_type=F32)
    return jnp.sum(before * onehot.astype(F32), axis=1).astype(jnp.int32)


def split3(x, axis):
    hi = lax.reduce_precision(x, exponent_bits=8, mantissa_bits=7)
    rest = x - hi
    mid = lax.reduce_precision(rest, exponent_bits=8, mantissa_bits=7)
    lo = rest - mid
    return jnp.concatenate([hi, mid, lo], axis=axis).astype(BF)


def split2(x, axis):
    hi = lax.reduce_precision(x, exponent_bits=8, mantissa_bits=7)
    return jnp.concatenate([hi, x - hi], axis=axis).astype(BF)


def join2(y, axis):
    a, b = jnp.split(y, 2, axis=axis)
    return a + b


def join3(y, axis):
    a, b, c = jnp.split(y, 3, axis=axis)
    return (a + b) + c


def clenshaw_constants(order):
    c1 = [(2 * l + 1) / (l + 1) for l in range(order + 1)]
    c2 = [l / (l + 1) for l in range(order + 2)]
    mu = [1.0] * (order + 1)
    for l in range(order - 1, -1, -1):
        mu[l] = c1[l] * mu[l + 1]
    gamma = [c2[l + 1] / (c1[l] * c1[l + 1]) for l in range(order - 1)]
    return mu, gamma


def expansion_terms(fine, strength, centre_pos, rel_targets):
    mu, gamma = clenshaw_constants(ORDER)
    ax = fine[:, 0] - centre_pos[:, 0][:, None]
    ay = fine[:, 1] - centre_pos[:, 1][:, None]
    az = fine[:, 2] - centre_pos[:, 2][:, None]
    bx, by, bz = rel_targets[:, 0], rel_targets[:, 1], rel_targets[:, 2]
    rs2 = ax * ax + ay * ay + az * az
    rt2 = bx * bx + by * by + bz * bz
    inv_rs2 = 1.0 / rs2
    scale = (strength * mu[0]) * lax.rsqrt(rs2)
    ax = ax * inv_rs2
    ay = ay * inv_rs2
    az = az * inv_rs2
    w = ax[:, :, None] * bx[:, None] + ay[:, :, None] * by[:, None] + az[:, :, None] * bz[:, None]
    rho2 = rt2[:, None] * inv_rs2[:, :, None]
    t_next = w + (1.0 / mu[ORDER - 1])
    t_after = jnp.ones_like(w)
    for level in range(ORDER - 2, -1, -1):
        t_now = (w * t_next + (1.0 / mu[level])) - gamma[level] * (rho2 * t_after)
        t_after, t_next = (t_next, t_now)
    return jnp.sum(scale[:, :, None] * t_next, axis=1)


def per_device(
    panel_nodes,
    density,
    crevice_routes,
    crevice_centre,
    centres,
    targets,
    centre_home,
    upsample,
    fine_weights,
):
    devices = lax.axis_size(("grp", "dev"))
    panels = crevice_routes.shape[0]
    fanout = crevice_routes.shape[1]
    centre_count = centres.shape[1]
    capacity = max(2, 2 * panels * fanout // devices)
    capacity_back = max(2, 2 * centre_count // devices)
    fine_count, nodes = upsample.shape
    pairs = panels * fanout
    slots = devices * capacity
    width = 4 * nodes

    coarse = jnp.concatenate(
        [panel_nodes.reshape(3, panels, nodes).transpose(1, 0, 2).reshape(panels, 3 * nodes),
         density.reshape(panels, nodes)],
        axis=1,
    )
    coarse_parts = jnp.concatenate([split3(coarse, 1)] * fanout, axis=0)
    ids1 = jnp.concatenate([crevice_centre[:, t] for t in range(fanout)]) + 1
    id_parts = jnp.stack([ids1 // 16, ids1 % 16], axis=1).astype(BF)
    rhs = jnp.concatenate([coarse_parts, id_parts], axis=1)

    destination = jnp.concatenate([crevice_routes[:, t] for t in range(fanout)])
    slot_index = destination * capacity + route_rank(destination, devices)
    place = (jnp.arange(slots, dtype=jnp.int32)[:, None] == slot_index[None, :]).astype(BF)
    placed = jnp.dot(place, rhs, preferred_element_type=F32)
    payload = join3(placed[:, : 3 * width], 1)
    slot_ids = 16.0 * placed[:, 3 * width] + placed[:, 3 * width + 1]
    outgoing = jnp.concatenate(
        [
            payload.reshape(devices, capacity * width),
            slot_ids.reshape(devices, capacity),
            jnp.zeros((devices, 2 * width - capacity), F32),
        ],
        axis=1,
    )

    incoming = lax.all_to_all(outgoing, ("grp", "dev"), split_axis=0, concat_axis=0, tiled=True)

    rows = capacity // 2
    block = incoming.reshape(devices, rows + 1, 2 * width)
    coarse_in = block[:, :rows, :].reshape(slots // 2, 2 * width)
    ids = jnp.round(block[:, rows, :capacity]).astype(jnp.int32)
    ids = ids.reshape(devices, rows, 2).transpose(2, 0, 1).reshape(2, slots // 2) - 1
    valid = ids >= 0
    pick = (jnp.arange(centre_count, dtype=jnp.int32)[None, :, None] == ids[:, None, :]).astype(BF)

    rel = targets.reshape(3, centre_count, nodes) - centres[:, :, None]
    data_rows = 3 + 3 * nodes
    padded_rows = -(-data_rows // 8) * 8
    centre_data = jnp.concatenate(
        [
            centres,
            rel.transpose(0, 2, 1).reshape(3 * nodes, centre_count),
            jnp.zeros((padded_rows - data_rows, centre_count), F32),
        ],
        axis=0,
    )
    gathered = join2(jnp.einsum("fg,pgs->pfs", split2(centre_data, 0), pick, preferred_element_type=F32), 1)
    slot_centre = gathered[:, :3]
    slot_targets = gathered[:, 3:data_rows].reshape(2, 3, nodes, slots // 2)

    eye_c = jnp.eye(4, dtype=F32)
    eye_p = jnp.eye(2, dtype=F32)
    refine_w = (
        eye_p[:, None, None, :, None, None] * eye_c[None, :, None, None, :, None] * upsample[None, None, :, None, None, :]
    ).reshape(2 * 4 * fine_count, 2 * width)
    upper = lax.dot_general(refine_w, coarse_in, (((1,), (1,)), ((), ())), precision=lax.Precision.HIGH)
    upper = upper.reshape(2, 4, fine_count, slots // 2)
    strength = upper[:, 3] * fine_weights[None, :, None]
    terms = expansion_terms(upper[:, :3], strength, slot_centre, slot_targets)
    terms = jnp.where(valid[:, None, :], terms, 0.0)

    potential = join2(jnp.einsum("pks,pgs->kg", split2(terms, 1), pick, preferred_element_type=F32), 0)

    home = centre_home.reshape(-1)
    back_index = home * capacity_back + route_rank(home, devices)
    back_place = (
        jnp.arange(devices * capacity_back, dtype=jnp.int32)[:, None] == back_index[None, :]
    ).astype(BF)
    sending = join3(
        lax.dot_general(back_place, split3(potential, 0), (((1,), (1,)), ((), ())), preferred_element_type=F32), 1
    )
    sending = sending.reshape(devices, capacity_back * nodes)
    returned = lax.all_to_all(sending, ("grp", "dev"), split_axis=0, concat_axis=0, tiled=True)
    return returned.reshape(-1)


def solution(mesh):
    placed = (
        P(None, ("grp", "dev")),
        P(("grp", "dev")),
        P(("grp", "dev"), None),
        P(("grp", "dev"), None),
        P(None, ("grp", "dev")),
        P(None, ("grp", "dev")),
        P(("grp", "dev"), None),
        P(),
        P(),
    )
    return jax.shard_map(
        per_device, mesh=mesh, in_specs=placed, out_specs=P(("grp", "dev")), check_vma=False
    )
```

```python
import jax
import jax.numpy as jnp
from jax import lax
from jax.sharding import PartitionSpec as P

ORDER = 8
HI = lax.Precision.HIGHEST
BF = jnp.bfloat16
F32 = jnp.float32


def route_rank(destination, count):
    rows = destination.shape[0]
    onehot = (destination[:, None] == jnp.arange(count, dtype=jnp.int32)[None, :]).astype(BF)
    lower = (jnp.arange(rows)[:, None] > jnp.arange(rows)[None, :]).astype(BF)
    before = jnp.dot(lower, onehot, preferred_element_type=F32)
    return jnp.sum(before * onehot.astype(F32), axis=1).astype(jnp.int32)


def split3(x, axis):
    hi = lax.reduce_precision(x, exponent_bits=8, mantissa_bits=7)
    rest = x - hi
    mid = lax.reduce_precision(rest, exponent_bits=8, mantissa_bits=7)
    lo = rest - mid
    return jnp.concatenate([hi, mid, lo], axis=axis).astype(BF)


def split2(x, axis):
    hi = lax.reduce_precision(x, exponent_bits=8, mantissa_bits=7)
    return jnp.concatenate([hi, x - hi], axis=axis).astype(BF)


def join2(y, axis):
    a, b = jnp.split(y, 2, axis=axis)
    return a + b


def join3(y, axis):
    a, b, c = jnp.split(y, 3, axis=axis)
    return (a + b) + c


def clenshaw_constants(order):
    c1 = [(2 * l + 1) / (l + 1) for l in range(order + 1)]
    c2 = [l / (l + 1) for l in range(order + 2)]
    mu = [1.0] * (order + 1)
    for l in range(order - 1, -1, -1):
        mu[l] = c1[l] * mu[l + 1]
    gamma = [c2[l + 1] / (c1[l] * c1[l + 1]) for l in range(order - 1)]
    return mu, gamma


def expansion_terms(fine, strength, centre_pos, rel_targets):
    mu, gamma = clenshaw_constants(ORDER)
    ax = fine[:, 0] - centre_pos[:, 0][:, None]
    ay = fine[:, 1] - centre_pos[:, 1][:, None]
    az = fine[:, 2] - centre_pos[:, 2][:, None]
    bx, by, bz = rel_targets[:, 0], rel_targets[:, 1], rel_targets[:, 2]
    rs2 = ax * ax + ay * ay + az * az
    rt2 = bx * bx + by * by + bz * bz
    inv_rs2 = 1.0 / rs2
    scale = (strength * mu[0]) * lax.rsqrt(rs2)
    ax = ax * inv_rs2
    ay = ay * inv_rs2
    az = az * inv_rs2
    w = ax[:, :, None] * bx[:, None] + ay[:, :, None] * by[:, None] + az[:, :, None] * bz[:, None]
    rho2 = rt2[:, None] * inv_rs2[:, :, None]
    t_next = w + (1.0 / mu[ORDER - 1])
    t_after = jnp.ones_like(w)
    for level in range(ORDER - 2, -1, -1):
        t_now = (w * t_next + (1.0 / mu[level])) - gamma[level] * (rho2 * t_after)
        t_after, t_next = (t_next, t_now)
    return jnp.sum(scale[:, :, None] * t_next, axis=1)


def per_device(
    panel_nodes,
    density,
    crevice_routes,
    crevice_centre,
    centres,
    targets,
    centre_home,
    upsample,
    fine_weights,
):
    devices = lax.axis_size(("grp", "dev"))
    panels = crevice_routes.shape[0]
    fanout = crevice_routes.shape[1]
    centre_count = centres.shape[1]
    capacity = max(2, 2 * panels * fanout // devices)
    capacity_back = max(2, 2 * centre_count // devices)
    fine_count, nodes = upsample.shape
    pairs = panels * fanout
    slots = devices * capacity
    width = 4 * nodes

    coarse = jnp.concatenate(
        [panel_nodes.reshape(3, panels, nodes).transpose(1, 0, 2).reshape(panels, 3 * nodes),
         density.reshape(panels, nodes)],
        axis=1,
    )
    coarse_parts = jnp.concatenate([split3(coarse, 1)] * fanout, axis=0)
    ids1 = jnp.concatenate([crevice_centre[:, t] for t in range(fanout)]) + 1
    id_parts = jnp.stack([ids1 // 16, ids1 % 16], axis=1).astype(BF)
    rhs = jnp.concatenate([coarse_parts, id_parts], axis=1)

    destination = jnp.concatenate([crevice_routes[:, t] for t in range(fanout)])
    slot_index = destination * capacity + route_rank(destination, devices)
    place = (jnp.arange(slots, dtype=jnp.int32)[:, None] == slot_index[None, :]).astype(BF)
    placed = jnp.dot(place, rhs, preferred_element_type=F32)
    payload = join3(placed[:, : 3 * width], 1)
    slot_ids = 16.0 * placed[:, 3 * width] + placed[:, 3 * width + 1]
    outgoing = jnp.concatenate(
        [
            payload.reshape(devices, capacity * width),
            slot_ids.reshape(devices, capacity),
            jnp.zeros((devices, 2 * width - capacity), F32),
        ],
        axis=1,
    )

    incoming = lax.all_to_all(outgoing, ("grp", "dev"), split_axis=0, concat_axis=0, tiled=True)

    rows = capacity // 2
    block = incoming.reshape(devices, rows + 1, 2 * width)
    coarse_in = block[:, :rows, :].reshape(slots // 2, 2 * width)
    ids = jnp.round(block[:, rows, :capacity]).astype(jnp.int32)
    ids = ids.reshape(devices, rows, 2).transpose(2, 0, 1).reshape(2, slots // 2) - 1
    valid = ids >= 0
    pick = (jnp.arange(centre_count, dtype=jnp.int32)[None, :, None] == ids[:, None, :]).astype(BF)

    home = centre_home.reshape(-1)
    back_index = home * capacity_back + route_rank(home, devices)
    rel = targets.reshape(3, centre_count, nodes) - centres[:, :, None]
    data_rows = 3 + 3 * nodes
    padded_rows = -(-(data_rows + 2) // 8) * 8
    centre_data = jnp.concatenate(
        [
            centres,
            rel.transpose(0, 2, 1).reshape(3 * nodes, centre_count),
            (back_index // 32).astype(F32)[None],
            (back_index % 32).astype(F32)[None],
            jnp.zeros((padded_rows - data_rows - 2, centre_count), F32),
        ],
        axis=0,
    )
    gathered = join2(jnp.einsum("fg,pgs->pfs", split2(centre_data, 0), pick, preferred_element_type=F32), 1)
    slot_centre = gathered[:, :3]
    slot_targets = gathered[:, 3:data_rows].reshape(2, 3, nodes, slots // 2)

    eye_c = jnp.eye(4, dtype=F32)
    eye_p = jnp.eye(2, dtype=F32)
    refine_w = (
        eye_p[:, None, None, :, None, None] * eye_c[None, :, None, None, :, None] * upsample[None, None, :, None, None, :]
    ).reshape(2 * 4 * fine_count, 2 * width)
    upper = lax.dot_general(refine_w, coarse_in, (((1,), (1,)), ((), ())), precision=lax.Precision.HIGH)
    upper = upper.reshape(2, 4, fine_count, slots // 2)
    strength = upper[:, 3] * fine_weights[None, :, None]
    terms = expansion_terms(upper[:, :3], strength, slot_centre, slot_targets)
    terms = jnp.where(valid[:, None, :], terms, 0.0)

    back_slot = 32.0 * gathered[:, data_rows] + gathered[:, data_rows + 1]
    to_back = (
        (jnp.arange(devices * capacity_back, dtype=F32)[:, None, None] == back_slot[None]) & valid[None]
    ).astype(BF)
    sending = join3(
        lax.dot_general(to_back, split3(terms, 1), (((1, 2), (0, 2)), ((), ())), preferred_element_type=F32), 1
    )
    sending = sending.reshape(devices, capacity_back * nodes)
    returned = lax.all_to_all(sending, ("grp", "dev"), split_axis=0, concat_axis=0, tiled=True)
    return returned.reshape(-1)


def solution(mesh):
    placed = (
        P(None, ("grp", "dev")),
        P(("grp", "dev")),
        P(("grp", "dev"), None),
        P(("grp", "dev"), None),
        P(None, ("grp", "dev")),
        P(None, ("grp", "dev")),
        P(("grp", "dev"), None),
        P(),
        P(),
    )
    return jax.shard_map(
        per_device, mesh=mesh, in_specs=placed, out_specs=P(("grp", "dev")), check_vma=False
    )
```

```python
import jax
import jax.numpy as jnp
from jax import lax
from jax.sharding import PartitionSpec as P

ORDER = 8
HI = lax.Precision.HIGHEST
BF = jnp.bfloat16
F32 = jnp.float32


def route_rank(destination, count):
    rows = destination.shape[0]
    onehot = (destination[:, None] == jnp.arange(count, dtype=jnp.int32)[None, :]).astype(BF)
    lower = (jnp.arange(rows)[:, None] > jnp.arange(rows)[None, :]).astype(BF)
    before = jnp.dot(lower, onehot, preferred_element_type=F32)
    return jnp.sum(before * onehot.astype(F32), axis=1).astype(jnp.int32)


def split3(x, axis):
    hi = lax.reduce_precision(x, exponent_bits=8, mantissa_bits=7)
    rest = x - hi
    mid = lax.reduce_precision(rest, exponent_bits=8, mantissa_bits=7)
    lo = rest - mid
    return jnp.concatenate([hi, mid, lo], axis=axis).astype(BF)


def split2(x, axis):
    hi = lax.reduce_precision(x, exponent_bits=8, mantissa_bits=7)
    return jnp.concatenate([hi, x - hi], axis=axis).astype(BF)


def join2(y, axis):
    a, b = jnp.split(y, 2, axis=axis)
    return a + b


def join3(y, axis):
    a, b, c = jnp.split(y, 3, axis=axis)
    return (a + b) + c


def clenshaw_constants(order):
    c1 = [(2 * l + 1) / (l + 1) for l in range(order + 1)]
    c2 = [l / (l + 1) for l in range(order + 2)]
    mu = [1.0] * (order + 1)
    for l in range(order - 1, -1, -1):
        mu[l] = c1[l] * mu[l + 1]
    gamma = [c2[l + 1] / (c1[l] * c1[l + 1]) for l in range(order - 1)]
    return mu, gamma


def expansion_terms(fine, strength, centre_pos, rel_targets):
    mu, gamma = clenshaw_constants(ORDER)
    ax = fine[:, 0] - centre_pos[:, 0][:, None]
    ay = fine[:, 1] - centre_pos[:, 1][:, None]
    az = fine[:, 2] - centre_pos[:, 2][:, None]
    bx, by, bz = rel_targets[:, 0], rel_targets[:, 1], rel_targets[:, 2]
    rs2 = ax * ax + ay * ay + az * az
    rt2 = bx * bx + by * by + bz * bz
    inv_rs2 = 1.0 / rs2
    scale = (strength * mu[0]) * lax.rsqrt(rs2)
    ax = ax * inv_rs2
    ay = ay * inv_rs2
    az = az * inv_rs2
    w = ax[:, :, None] * bx[:, None] + ay[:, :, None] * by[:, None] + az[:, :, None] * bz[:, None]
    rho2 = rt2[:, None] * inv_rs2[:, :, None]
    t_next = w + (1.0 / mu[ORDER - 1])
    t_after = jnp.ones_like(w)
    for level in range(ORDER - 2, -1, -1):
        t_now = (w * t_next + (1.0 / mu[level])) - gamma[level] * (rho2 * t_after)
        t_after, t_next = (t_next, t_now)
    return jnp.sum(scale[:, :, None] * t_next, axis=1)


def per_device(
    panel_nodes,
    density,
    crevice_routes,
    crevice_centre,
    centres,
    targets,
    centre_home,
    upsample,
    fine_weights,
):
    devices = lax.axis_size(("grp", "dev"))
    panels = crevice_routes.shape[0]
    fanout = crevice_routes.shape[1]
    centre_count = centres.shape[1]
    capacity = max(2, 2 * panels * fanout // devices)
    capacity_back = max(2, 2 * centre_count // devices)
    fine_count, nodes = upsample.shape
    pairs = panels * fanout
    slots = devices * capacity
    width = 4 * nodes

    coarse = jnp.concatenate(
        [panel_nodes.reshape(3, panels, nodes).transpose(1, 0, 2).reshape(panels, 3 * nodes),
         density.reshape(panels, nodes)],
        axis=1,
    )
    coarse_parts = jnp.concatenate([split3(coarse, 1)] * fanout, axis=0)
    ids1 = crevice_centre.T.reshape(pairs) + 1
    id_parts = jnp.stack([ids1 // 16, ids1 % 16], axis=1).astype(BF)
    rhs = jnp.concatenate([coarse_parts, id_parts], axis=1)

    destination = crevice_routes.T.reshape(pairs)
    slot_index = destination * capacity + route_rank(destination, devices)
    place = (jnp.arange(slots, dtype=jnp.int32)[:, None] == slot_index[None, :]).astype(BF)
    placed = jnp.dot(place, rhs, preferred_element_type=F32)
    payload = join3(placed[:, : 3 * width], 1)
    slot_ids = 16.0 * placed[:, 3 * width] + placed[:, 3 * width + 1]
    outgoing = jnp.concatenate(
        [
            payload.reshape(devices, capacity * width),
            slot_ids.reshape(devices, capacity),
            jnp.zeros((devices, 2 * width - capacity), F32),
        ],
        axis=1,
    )

    incoming = lax.all_to_all(outgoing, ("grp", "dev"), split_axis=0, concat_axis=0, tiled=True)

    rows = capacity // 2
    block = incoming.reshape(devices, rows + 1, 2 * width)
    coarse_in = block[:, :rows, :].reshape(slots // 2, 2 * width)
    ids = jnp.round(block[:, rows, :capacity]).astype(jnp.int32)
    ids = ids.reshape(devices, rows, 2).transpose(2, 0, 1).reshape(2, slots // 2) - 1
    valid = ids >= 0
    pick = (jnp.arange(centre_count, dtype=jnp.int32)[None, :, None] == ids[:, None, :]).astype(BF)

    rel = targets.reshape(3, centre_count, nodes) - centres[:, :, None]
    data_rows = 3 + 3 * nodes
    padded_rows = -(-data_rows // 8) * 8
    centre_data = jnp.concatenate(
        [
            centres,
            rel.transpose(0, 2, 1).reshape(3 * nodes, centre_count),
            jnp.zeros((padded_rows - data_rows, centre_count), F32),
        ],
        axis=0,
    )
    gathered = join2(jnp.einsum("fg,pgs->pfs", split2(centre_data, 0), pick, preferred_element_type=F32), 1)
    slot_centre = gathered[:, :3]
    slot_targets = gathered[:, 3:data_rows].reshape(2, 3, nodes, slots // 2)

    eye_c = jnp.eye(4, dtype=F32)
    eye_p = jnp.eye(2, dtype=F32)
    refine_w = (
        eye_p[:, None, None, :, None, None] * eye_c[None, :, None, None, :, None] * upsample[None, None, :, None, None, :]
    ).reshape(2 * 4 * fine_count, 2 * width)
    upper = lax.dot_general(refine_w, coarse_in, (((1,), (1,)), ((), ())), precision=lax.Precision.HIGH)
    upper = upper.reshape(2, 4, fine_count, slots // 2)
    strength = upper[:, 3] * fine_weights[None, :, None]
    terms = expansion_terms(upper[:, :3], strength, slot_centre, slot_targets)
    terms = jnp.where(valid[:, None, :], terms, 0.0)

    potential = join2(jnp.einsum("pks,pgs->kg", split2(terms, 1), pick, preferred_element_type=F32), 0)

    home = centre_home.reshape(-1)
    back_index = home * capacity_back + route_rank(home, devices)
    back_place = (
        jnp.arange(devices * capacity_back, dtype=jnp.int32)[:, None] == back_index[None, :]
    ).astype(BF)
    sending = join3(
        lax.dot_general(back_place, split3(potential, 0), (((1,), (1,)), ((), ())), preferred_element_type=F32), 1
    )
    sending = sending.reshape(devices, capacity_back * nodes)
    returned = lax.all_to_all(sending, ("grp", "dev"), split_axis=0, concat_axis=0, tiled=True)
    return returned.reshape(-1)


def solution(mesh):
    placed = (
        P(None, ("grp", "dev")),
        P(("grp", "dev")),
        P(("grp", "dev"), None),
        P(("grp", "dev"), None),
        P(None, ("grp", "dev")),
        P(None, ("grp", "dev")),
        P(("grp", "dev"), None),
        P(),
        P(),
    )
    return jax.shard_map(
        per_device, mesh=mesh, in_specs=placed, out_specs=P(("grp", "dev")), check_vma=False
    )
```

```python
import jax
import jax.numpy as jnp
from jax import lax
from jax.sharding import PartitionSpec as P

ORDER = 8
HI = lax.Precision.HIGHEST
BF = jnp.bfloat16
F32 = jnp.float32


def route_rank(destination, count):
    rows = destination.shape[0]
    onehot = (destination[:, None] == jnp.arange(count, dtype=jnp.int32)[None, :]).astype(BF)
    lower = (jnp.arange(rows)[:, None] > jnp.arange(rows)[None, :]).astype(BF)
    before = jnp.dot(lower, onehot, preferred_element_type=F32)
    return jnp.sum(before * onehot.astype(F32), axis=1).astype(jnp.int32)


def split3(x, axis):
    hi = lax.reduce_precision(x, exponent_bits=8, mantissa_bits=7)
    rest = x - hi
    mid = lax.reduce_precision(rest, exponent_bits=8, mantissa_bits=7)
    lo = rest - mid
    return jnp.concatenate([hi, mid, lo], axis=axis).astype(BF)


def split2(x, axis):
    hi = lax.reduce_precision(x, exponent_bits=8, mantissa_bits=7)
    return jnp.concatenate([hi, x - hi], axis=axis).astype(BF)


def join2(y, axis):
    a, b = jnp.split(y, 2, axis=axis)
    return a + b


def join3(y, axis):
    a, b, c = jnp.split(y, 3, axis=axis)
    return (a + b) + c


def clenshaw_constants(order):
    c1 = [(2 * l + 1) / (l + 1) for l in range(order + 1)]
    c2 = [l / (l + 1) for l in range(order + 2)]
    mu = [1.0] * (order + 1)
    for l in range(order - 1, -1, -1):
        mu[l] = c1[l] * mu[l + 1]
    gamma = [c2[l + 1] / (c1[l] * c1[l + 1]) for l in range(order - 1)]
    return mu, gamma


def expansion_terms(fine, strength, centre_pos, rel_targets):
    mu, gamma = clenshaw_constants(ORDER)
    ax = fine[:, 0] - centre_pos[:, 0][:, None]
    ay = fine[:, 1] - centre_pos[:, 1][:, None]
    az = fine[:, 2] - centre_pos[:, 2][:, None]
    bx, by, bz = rel_targets[:, 0], rel_targets[:, 1], rel_targets[:, 2]
    rs2 = ax * ax + ay * ay + az * az
    rt2 = bx * bx + by * by + bz * bz
    inv_rs2 = 1.0 / rs2
    scale = (strength * mu[0]) * lax.rsqrt(rs2)
    ax = ax * inv_rs2
    ay = ay * inv_rs2
    az = az * inv_rs2
    w = ax[:, :, None] * bx[:, None] + ay[:, :, None] * by[:, None] + az[:, :, None] * bz[:, None]
    rho2 = rt2[:, None] * inv_rs2[:, :, None]
    t_next = w + (1.0 / mu[ORDER - 1])
    t_after = jnp.ones_like(w)
    for level in range(ORDER - 2, -1, -1):
        t_now = (w * t_next + (1.0 / mu[level])) - gamma[level] * (rho2 * t_after)
        t_after, t_next = (t_next, t_now)
    return jnp.sum(scale[:, :, None] * t_next, axis=1)


def per_device(
    panel_nodes,
    density,
    crevice_routes,
    crevice_centre,
    centres,
    targets,
    centre_home,
    upsample,
    fine_weights,
):
    devices = lax.axis_size(("grp", "dev"))
    panels = crevice_routes.shape[0]
    fanout = crevice_routes.shape[1]
    centre_count = centres.shape[1]
    capacity = max(2, 2 * panels * fanout // devices)
    capacity_back = max(2, 2 * centre_count // devices)
    fine_count, nodes = upsample.shape
    pairs = panels * fanout
    slots = devices * capacity
    width = 4 * nodes

    coarse = (
        lax.optimization_barrier(jnp.concatenate([panel_nodes, density[None]], axis=0))
        .reshape(4, panels, nodes)
        .transpose(1, 0, 2)
        .reshape(panels, width)
    )
    coarse_parts = jnp.concatenate([split3(coarse, 1)] * fanout, axis=0)
    ids1 = crevice_centre.T.reshape(pairs) + 1
    id_parts = jnp.stack([ids1 // 16, ids1 % 16], axis=1).astype(BF)
    rhs = jnp.concatenate([coarse_parts, id_parts], axis=1)

    destination = crevice_routes.T.reshape(pairs)
    slot_index = destination * capacity + route_rank(destination, devices)
    place = (jnp.arange(slots, dtype=jnp.int32)[:, None] == slot_index[None, :]).astype(BF)
    placed = jnp.dot(place, rhs, preferred_element_type=F32)
    payload = join3(placed[:, : 3 * width], 1)
    slot_ids = 16.0 * placed[:, 3 * width] + placed[:, 3 * width + 1]
    outgoing = jnp.concatenate(
        [
            payload.reshape(devices, capacity * width),
            slot_ids.reshape(devices, capacity),
            jnp.zeros((devices, 2 * width - capacity), F32),
        ],
        axis=1,
    )

    incoming = lax.all_to_all(outgoing, ("grp", "dev"), split_axis=0, concat_axis=0, tiled=True)

    rows = capacity // 2
    block = incoming.reshape(devices, rows + 1, 2 * width)
    coarse_in = block[:, :rows, :].reshape(slots // 2, 2 * width)
    ids = jnp.round(block[:, rows, :capacity]).astype(jnp.int32)
    ids = ids.reshape(devices, rows, 2).transpose(2, 0, 1).reshape(2, slots // 2) - 1
    valid = ids >= 0
    pick = (jnp.arange(centre_count, dtype=jnp.int32)[None, :, None] == ids[:, None, :]).astype(BF)

    rel = targets.reshape(3, centre_count, nodes) - centres[:, :, None]
    data_rows = 3 + 3 * nodes
    padded_rows = -(-data_rows // 8) * 8
    centre_data = jnp.concatenate(
        [
            centres,
            rel.transpose(0, 2, 1).reshape(3 * nodes, centre_count),
            jnp.zeros((padded_rows - data_rows, centre_count), F32),
        ],
        axis=0,
    )
    gathered = join2(jnp.einsum("fg,pgs->pfs", split2(centre_data, 0), pick, preferred_element_type=F32), 1)
    slot_centre = gathered[:, :3]
    slot_targets = gathered[:, 3:data_rows].reshape(2, 3, nodes, slots // 2)

    eye_c = jnp.eye(4, dtype=F32)
    eye_p = jnp.eye(2, dtype=F32)
    refine_w = (
        eye_p[:, None, None, :, None, None] * eye_c[None, :, None, None, :, None] * upsample[None, None, :, None, None, :]
    ).reshape(2 * 4 * fine_count, 2 * width)
    upper = lax.dot_general(refine_w, coarse_in, (((1,), (1,)), ((), ())), precision=lax.Precision.HIGH)
    upper = upper.reshape(2, 4, fine_count, slots // 2)
    strength = upper[:, 3] * fine_weights[None, :, None]
    terms = expansion_terms(upper[:, :3], strength, slot_centre, slot_targets)
    terms = jnp.where(valid[:, None, :], terms, 0.0)

    potential = join2(jnp.einsum("pks,pgs->kg", split2(terms, 1), pick, preferred_element_type=F32), 0)

    home = centre_home.reshape(-1)
    back_index = home * capacity_back + route_rank(home, devices)
    back_place = (
        jnp.arange(devices * capacity_back, dtype=jnp.int32)[:, None] == back_index[None, :]
    ).astype(BF)
    sending = join3(
        lax.dot_general(back_place, split3(potential, 0), (((1,), (1,)), ((), ())), preferred_element_type=F32), 1
    )
    sending = sending.reshape(devices, capacity_back * nodes)
    returned = lax.all_to_all(sending, ("grp", "dev"), split_axis=0, concat_axis=0, tiled=True)
    return returned.reshape(-1)


def solution(mesh):
    placed = (
        P(None, ("grp", "dev")),
        P(("grp", "dev")),
        P(("grp", "dev"), None),
        P(("grp", "dev"), None),
        P(None, ("grp", "dev")),
        P(None, ("grp", "dev")),
        P(("grp", "dev"), None),
        P(),
        P(),
    )
    return jax.shard_map(
        per_device, mesh=mesh, in_specs=placed, out_specs=P(("grp", "dev")), check_vma=False
    )
```

```python
import jax
import jax.numpy as jnp
from jax import lax
from jax.sharding import PartitionSpec as P

ORDER = 8
HI = lax.Precision.HIGHEST
BF = jnp.bfloat16
F32 = jnp.float32


def route_rank(destination, count):
    rows = destination.shape[0]
    onehot = (destination[:, None] == jnp.arange(count, dtype=jnp.int32)[None, :]).astype(BF)
    lower = (jnp.arange(rows)[:, None] > jnp.arange(rows)[None, :]).astype(BF)
    before = jnp.dot(lower, onehot, preferred_element_type=F32)
    return jnp.sum(before * onehot.astype(F32), axis=1).astype(jnp.int32)


def split3(x, axis):
    hi = lax.reduce_precision(x, exponent_bits=8, mantissa_bits=7)
    rest = x - hi
    mid = lax.reduce_precision(rest, exponent_bits=8, mantissa_bits=7)
    lo = rest - mid
    return jnp.concatenate([hi, mid, lo], axis=axis).astype(BF)


def split2(x, axis):
    hi = lax.reduce_precision(x, exponent_bits=8, mantissa_bits=7)
    return jnp.concatenate([hi, x - hi], axis=axis).astype(BF)


def join2(y, axis):
    a, b = jnp.split(y, 2, axis=axis)
    return a + b


def join3(y, axis):
    a, b, c = jnp.split(y, 3, axis=axis)
    return (a + b) + c


def clenshaw_constants(order):
    c1 = [(2 * l + 1) / (l + 1) for l in range(order + 1)]
    c2 = [l / (l + 1) for l in range(order + 2)]
    mu = [1.0] * (order + 1)
    for l in range(order - 1, -1, -1):
        mu[l] = c1[l] * mu[l + 1]
    gamma = [c2[l + 1] / (c1[l] * c1[l + 1]) for l in range(order - 1)]
    return mu, gamma


def expansion_terms(fine, strength, centre_pos, rel_targets):
    mu, gamma = clenshaw_constants(ORDER)
    ax = fine[:, 0] - centre_pos[:, 0][:, None]
    ay = fine[:, 1] - centre_pos[:, 1][:, None]
    az = fine[:, 2] - centre_pos[:, 2][:, None]
    bx, by, bz = rel_targets[:, 0], rel_targets[:, 1], rel_targets[:, 2]
    rs2 = ax * ax + ay * ay + az * az
    rt2 = bx * bx + by * by + bz * bz
    inv_rs2 = 1.0 / rs2
    scale = (strength * mu[0]) * lax.rsqrt(rs2)
    ax = ax * inv_rs2
    ay = ay * inv_rs2
    az = az * inv_rs2
    w = ax[:, :, None] * bx[:, None] + ay[:, :, None] * by[:, None] + az[:, :, None] * bz[:, None]
    rho2 = rt2[:, None] * inv_rs2[:, :, None]
    t_next = w + (1.0 / mu[ORDER - 1])
    t_after = jnp.ones_like(w)
    for level in range(ORDER - 2, -1, -1):
        t_now = (w * t_next + (1.0 / mu[level])) - gamma[level] * (rho2 * t_after)
        t_after, t_next = (t_next, t_now)
    return jnp.sum(scale[:, :, None] * t_next, axis=1)


def per_device(
    panel_nodes,
    density,
    crevice_routes,
    crevice_centre,
    centres,
    targets,
    centre_home,
    upsample,
    fine_weights,
):
    devices = lax.axis_size(("grp", "dev"))
    panels = crevice_routes.shape[0]
    fanout = crevice_routes.shape[1]
    centre_count = centres.shape[1]
    capacity = max(2, 2 * panels * fanout // devices)
    capacity_back = max(2, 2 * centre_count // devices)
    fine_count, nodes = upsample.shape
    pairs = panels * fanout
    slots = devices * capacity
    width = 4 * nodes

    coarse = (
        lax.optimization_barrier(jnp.concatenate([panel_nodes, density[None]], axis=0))
        .reshape(4, panels, nodes)
        .transpose(1, 0, 2)
        .reshape(panels, width)
    )
    coarse_parts = jnp.concatenate([split3(coarse, 1)] * fanout, axis=0)
    ids1 = crevice_centre.T.reshape(pairs) + 1
    id_parts = jnp.stack([ids1 // 16, ids1 % 16], axis=1).astype(BF)
    rhs = jnp.concatenate([coarse_parts, id_parts], axis=1)

    destination = crevice_routes.T.reshape(pairs)
    slot_index = destination * capacity + route_rank(destination, devices)
    place = (jnp.arange(slots, dtype=jnp.int32)[:, None] == slot_index[None, :]).astype(BF)
    placed = jnp.dot(place, rhs, preferred_element_type=F32)
    payload = join3(placed[:, : 3 * width], 1)
    slot_ids = 16.0 * placed[:, 3 * width] + placed[:, 3 * width + 1]
    outgoing = (
        jnp.zeros((devices, capacity * width + 2 * width), F32)
        .at[:, : capacity * width].set(payload.reshape(devices, capacity * width))
        .at[:, capacity * width : capacity * width + capacity].set(slot_ids.reshape(devices, capacity))
    )

    incoming = lax.all_to_all(outgoing, ("grp", "dev"), split_axis=0, concat_axis=0, tiled=True)

    rows = capacity // 2
    block = incoming.reshape(devices, rows + 1, 2 * width)
    coarse_in = block[:, :rows, :].reshape(slots // 2, 2 * width)
    ids = jnp.round(block[:, rows, :capacity]).astype(jnp.int32)
    ids = ids.reshape(devices, rows, 2).transpose(2, 0, 1).reshape(2, slots // 2) - 1
    valid = ids >= 0
    pick = (jnp.arange(centre_count, dtype=jnp.int32)[None, :, None] == ids[:, None, :]).astype(BF)

    rel = targets.reshape(3, centre_count, nodes) - centres[:, :, None]
    data_rows = 3 + 3 * nodes
    padded_rows = -(-data_rows // 8) * 8
    centre_data = jnp.concatenate(
        [
            centres,
            rel.transpose(0, 2, 1).reshape(3 * nodes, centre_count),
            jnp.zeros((padded_rows - data_rows, centre_count), F32),
        ],
        axis=0,
    )
    gathered = join2(jnp.einsum("fg,pgs->pfs", split2(centre_data, 0), pick, preferred_element_type=F32), 1)
    slot_centre = gathered[:, :3]
    slot_targets = gathered[:, 3:data_rows].reshape(2, 3, nodes, slots // 2)

    eye_c = jnp.eye(4, dtype=F32)
    eye_p = jnp.eye(2, dtype=F32)
    refine_w = (
        eye_p[:, None, None, :, None, None] * eye_c[None, :, None, None, :, None] * upsample[None, None, :, None, None, :]
    ).reshape(2 * 4 * fine_count, 2 * width)
    upper = lax.dot_general(refine_w, coarse_in, (((1,), (1,)), ((), ())), precision=lax.Precision.HIGH)
    upper = upper.reshape(2, 4, fine_count, slots // 2)
    strength = upper[:, 3] * fine_weights[None, :, None]
    terms = expansion_terms(upper[:, :3], strength, slot_centre, slot_targets)
    terms = jnp.where(valid[:, None, :], terms, 0.0)

    potential = join2(jnp.einsum("pks,pgs->kg", split2(terms, 1), pick, preferred_element_type=F32), 0)

    home = centre_home.reshape(-1)
    back_index = home * capacity_back + route_rank(home, devices)
    back_place = (
        jnp.arange(devices * capacity_back, dtype=jnp.int32)[:, None] == back_index[None, :]
    ).astype(BF)
    sending = join3(
        lax.dot_general(back_place, split3(potential, 0), (((1,), (1,)), ((), ())), preferred_element_type=F32), 1
    )
    sending = sending.reshape(devices, capacity_back * nodes)
    returned = lax.all_to_all(sending, ("grp", "dev"), split_axis=0, concat_axis=0, tiled=True)
    return returned.reshape(-1)


def solution(mesh):
    placed = (
        P(None, ("grp", "dev")),
        P(("grp", "dev")),
        P(("grp", "dev"), None),
        P(("grp", "dev"), None),
        P(None, ("grp", "dev")),
        P(None, ("grp", "dev")),
        P(("grp", "dev"), None),
        P(),
        P(),
    )
    return jax.shard_map(
        per_device, mesh=mesh, in_specs=placed, out_specs=P(("grp", "dev")), check_vma=False
    )
```

```python
import functools

import jax
import jax.numpy as jnp
from jax import lax
from jax.sharding import PartitionSpec as P

ORDER = 8
HI = lax.Precision.HIGHEST
BF = jnp.bfloat16
F32 = jnp.float32


def route_rank(destination, count):
    rows = destination.shape[0]
    onehot = (destination[:, None] == jnp.arange(count, dtype=jnp.int32)[None, :]).astype(BF)
    lower = (jnp.arange(rows)[:, None] > jnp.arange(rows)[None, :]).astype(BF)
    before = jnp.dot(lower, onehot, preferred_element_type=F32)
    return jnp.sum(before * onehot.astype(F32), axis=1).astype(jnp.int32)


def split3(x, axis):
    hi = lax.reduce_precision(x, exponent_bits=8, mantissa_bits=7)
    rest = x - hi
    mid = lax.reduce_precision(rest, exponent_bits=8, mantissa_bits=7)
    lo = rest - mid
    return jnp.concatenate([hi, mid, lo], axis=axis).astype(BF)


def split2(x, axis):
    hi = lax.reduce_precision(x, exponent_bits=8, mantissa_bits=7)
    return jnp.concatenate([hi, x - hi], axis=axis).astype(BF)


def join2(y, axis):
    a, b = jnp.split(y, 2, axis=axis)
    return a + b


def join3(y, axis):
    a, b, c = jnp.split(y, 3, axis=axis)
    return (a + b) + c


def clenshaw_constants(order):
    c1 = [(2 * l + 1) / (l + 1) for l in range(order + 1)]
    c2 = [l / (l + 1) for l in range(order + 2)]
    mu = [1.0] * (order + 1)
    for l in range(order - 1, -1, -1):
        mu[l] = c1[l] * mu[l + 1]
    gamma = [c2[l + 1] / (c1[l] * c1[l + 1]) for l in range(order - 1)]
    return mu, gamma


def expansion_terms(fine, strength, centre_pos, rel_targets):
    mu, gamma = clenshaw_constants(ORDER)
    ax = fine[:, 0] - centre_pos[:, 0][:, None]
    ay = fine[:, 1] - centre_pos[:, 1][:, None]
    az = fine[:, 2] - centre_pos[:, 2][:, None]
    bx, by, bz = rel_targets[:, 0], rel_targets[:, 1], rel_targets[:, 2]
    rs2 = ax * ax + ay * ay + az * az
    rt2 = bx * bx + by * by + bz * bz
    inv_rs2 = 1.0 / rs2
    scale = (strength * mu[0]) * lax.rsqrt(rs2)
    ax = ax * inv_rs2
    ay = ay * inv_rs2
    az = az * inv_rs2
    w = ax[:, :, None] * bx[:, None] + ay[:, :, None] * by[:, None] + az[:, :, None] * bz[:, None]
    rho2 = rt2[:, None] * inv_rs2[:, :, None]
    t_next = w + (1.0 / mu[ORDER - 1])
    t_after = jnp.ones_like(w)
    for level in range(ORDER - 2, -1, -1):
        t_now = (w * t_next + (1.0 / mu[level])) - gamma[level] * (rho2 * t_after)
        t_after, t_next = (t_next, t_now)
    return jnp.sum(scale[:, :, None] * t_next, axis=1)


def per_device(
    panel_nodes,
    density,
    crevice_routes,
    crevice_centre,
    centres,
    targets,
    centre_home,
    upsample,
    fine_weights,
):
    devices = lax.axis_size(("grp", "dev"))
    panels = crevice_routes.shape[0]
    fanout = crevice_routes.shape[1]
    centre_count = centres.shape[1]
    capacity = max(2, 2 * panels * fanout // devices)
    capacity_back = max(2, 2 * centre_count // devices)
    fine_count, nodes = upsample.shape
    pairs = panels * fanout
    slots = devices * capacity
    width = 4 * nodes

    coarse = (
        lax.optimization_barrier(jnp.concatenate([panel_nodes, density[None]], axis=0))
        .reshape(4, panels, nodes)
        .transpose(1, 0, 2)
        .reshape(panels, width)
    )
    ids1 = crevice_centre.T + 1
    destination = crevice_routes.T.reshape(pairs)
    slot_index = destination * capacity + route_rank(destination, devices)
    slot_t = slot_index.reshape(fanout, panels)
    extra = [ids1[t] // 16 for t in range(fanout)] + [ids1[t] % 16 for t in range(fanout)]
    extra += [slot_t[t] // 64 for t in range(fanout)] + [slot_t[t] % 64 for t in range(fanout)]
    rhs = jnp.concatenate([split3(coarse, 1), jnp.stack(extra, axis=1).astype(BF)], axis=1)
    slot_iota = jnp.arange(slots, dtype=jnp.int32)[:, None]
    place = functools.reduce(jnp.logical_or, [slot_iota == slot_t[t][None, :] for t in range(fanout)]).astype(BF)
    placed = jnp.dot(place, rhs, preferred_element_type=F32)
    payload = join3(placed[:, : 3 * width], 1)
    col = 3 * width
    slot_here = jnp.arange(slots, dtype=F32)
    slot_ids = jnp.zeros((slots,), F32)
    for t in range(fanout):
        id_t = 16.0 * placed[:, col + t] + placed[:, col + fanout + t]
        slot_of_t = 64.0 * placed[:, col + 2 * fanout + t] + placed[:, col + 3 * fanout + t]
        slot_ids = jnp.where(slot_of_t == slot_here, id_t, slot_ids)
    outgoing = jnp.concatenate(
        [
            payload.reshape(devices, capacity * width),
            slot_ids.reshape(devices, capacity),
            jnp.zeros((devices, 2 * width - capacity), F32),
        ],
        axis=1,
    )

    incoming = lax.all_to_all(outgoing, ("grp", "dev"), split_axis=0, concat_axis=0, tiled=True)

    rows = capacity // 2
    block = incoming.reshape(devices, rows + 1, 2 * width)
    coarse_in = block[:, :rows, :].reshape(slots // 2, 2 * width)
    ids = jnp.round(block[:, rows, :capacity]).astype(jnp.int32)
    ids = ids.reshape(devices, rows, 2).transpose(2, 0, 1).reshape(2, slots // 2) - 1
    valid = ids >= 0
    pick = (jnp.arange(centre_count, dtype=jnp.int32)[None, :, None] == ids[:, None, :]).astype(BF)

    rel = targets.reshape(3, centre_count, nodes) - centres[:, :, None]
    data_rows = 3 + 3 * nodes
    padded_rows = -(-data_rows // 8) * 8
    centre_data = jnp.concatenate(
        [
            centres,
            rel.transpose(0, 2, 1).reshape(3 * nodes, centre_count),
            jnp.zeros((padded_rows - data_rows, centre_count), F32),
        ],
        axis=0,
    )
    gathered = join2(jnp.einsum("fg,pgs->pfs", split2(centre_data, 0), pick, preferred_element_type=F32), 1)
    slot_centre = gathered[:, :3]
    slot_targets = gathered[:, 3:data_rows].reshape(2, 3, nodes, slots // 2)

    eye_c = jnp.eye(4, dtype=F32)
    eye_p = jnp.eye(2, dtype=F32)
    refine_w = (
        eye_p[:, None, None, :, None, None] * eye_c[None, :, None, None, :, None] * upsample[None, None, :, None, None, :]
    ).reshape(2 * 4 * fine_count, 2 * width)
    upper = lax.dot_general(refine_w, coarse_in, (((1,), (1,)), ((), ())), precision=lax.Precision.HIGH)
    upper = upper.reshape(2, 4, fine_count, slots // 2)
    strength = upper[:, 3] * fine_weights[None, :, None]
    terms = expansion_terms(upper[:, :3], strength, slot_centre, slot_targets)
    terms = jnp.where(valid[:, None, :], terms, 0.0)

    potential = join2(jnp.einsum("pks,pgs->kg", split2(terms, 1), pick, preferred_element_type=F32), 0)

    home = centre_home.reshape(-1)
    back_index = home * capacity_back + route_rank(home, devices)
    back_place = (
        jnp.arange(devices * capacity_back, dtype=jnp.int32)[:, None] == back_index[None, :]
    ).astype(BF)
    sending = join3(
        lax.dot_general(back_place, split3(potential, 0), (((1,), (1,)), ((), ())), preferred_element_type=F32), 1
    )
    sending = sending.reshape(devices, capacity_back * nodes)
    returned = lax.all_to_all(sending, ("grp", "dev"), split_axis=0, concat_axis=0, tiled=True)
    return returned.reshape(-1)


def solution(mesh):
    placed = (
        P(None, ("grp", "dev")),
        P(("grp", "dev")),
        P(("grp", "dev"), None),
        P(("grp", "dev"), None),
        P(None, ("grp", "dev")),
        P(None, ("grp", "dev")),
        P(("grp", "dev"), None),
        P(),
        P(),
    )
    return jax.shard_map(
        per_device, mesh=mesh, in_specs=placed, out_specs=P(("grp", "dev")), check_vma=False
    )
```

```python
import functools

import jax
import jax.numpy as jnp
from jax import lax
from jax.sharding import PartitionSpec as P

ORDER = 8
HI = lax.Precision.HIGHEST
BF = jnp.bfloat16
F32 = jnp.float32


def route_rank(destination, count):
    rows = destination.shape[0]
    onehot = (destination[:, None] == jnp.arange(count, dtype=jnp.int32)[None, :]).astype(BF)
    lower = (jnp.arange(rows)[:, None] > jnp.arange(rows)[None, :]).astype(BF)
    before = jnp.dot(lower, onehot, preferred_element_type=F32)
    return jnp.sum(before * onehot.astype(F32), axis=1).astype(jnp.int32)


def split3(x, axis):
    hi = lax.reduce_precision(x, exponent_bits=8, mantissa_bits=7)
    rest = x - hi
    mid = lax.reduce_precision(rest, exponent_bits=8, mantissa_bits=7)
    lo = rest - mid
    return jnp.concatenate([hi, mid, lo], axis=axis).astype(BF)


def split2(x, axis):
    hi = lax.reduce_precision(x, exponent_bits=8, mantissa_bits=7)
    return jnp.concatenate([hi, x - hi], axis=axis).astype(BF)


def join2(y, axis):
    a, b = jnp.split(y, 2, axis=axis)
    return a + b


def join3(y, axis):
    a, b, c = jnp.split(y, 3, axis=axis)
    return (a + b) + c


def clenshaw_constants(order):
    c1 = [(2 * l + 1) / (l + 1) for l in range(order + 1)]
    c2 = [l / (l + 1) for l in range(order + 2)]
    mu = [1.0] * (order + 1)
    for l in range(order - 1, -1, -1):
        mu[l] = c1[l] * mu[l + 1]
    gamma = [c2[l + 1] / (c1[l] * c1[l + 1]) for l in range(order - 1)]
    return mu, gamma


def expansion_terms(fine, strength, centre_pos, rel_targets):
    mu, gamma = clenshaw_constants(ORDER)
    ax = fine[:, 0] - centre_pos[:, 0][:, None]
    ay = fine[:, 1] - centre_pos[:, 1][:, None]
    az = fine[:, 2] - centre_pos[:, 2][:, None]
    bx, by, bz = rel_targets[:, 0], rel_targets[:, 1], rel_targets[:, 2]
    rs2 = ax * ax + ay * ay + az * az
    rt2 = bx * bx + by * by + bz * bz
    inv_rs2 = 1.0 / rs2
    scale = (strength * mu[0]) * lax.rsqrt(rs2)
    ax = ax * inv_rs2
    ay = ay * inv_rs2
    az = az * inv_rs2
    w = ax[:, :, None] * bx[:, None] + ay[:, :, None] * by[:, None] + az[:, :, None] * bz[:, None]
    rho2 = rt2[:, None] * inv_rs2[:, :, None]
    t_next = w + (1.0 / mu[ORDER - 1])
    t_after = jnp.ones_like(w)
    for level in range(ORDER - 2, -1, -1):
        t_now = (w * t_next + (1.0 / mu[level])) - gamma[level] * (rho2 * t_after)
        t_after, t_next = (t_next, t_now)
    return jnp.sum(scale[:, :, None] * t_next, axis=1)


def per_device(
    panel_nodes,
    density,
    crevice_routes,
    crevice_centre,
    centres,
    targets,
    centre_home,
    upsample,
    fine_weights,
):
    devices = lax.axis_size(("grp", "dev"))
    panels = crevice_routes.shape[0]
    fanout = crevice_routes.shape[1]
    centre_count = centres.shape[1]
    capacity = max(2, 2 * panels * fanout // devices)
    capacity_back = max(2, 2 * centre_count // devices)
    fine_count, nodes = upsample.shape
    pairs = panels * fanout
    slots = devices * capacity
    width = 4 * nodes

    coarse = (
        lax.optimization_barrier(jnp.concatenate([panel_nodes, density[None]], axis=0))
        .reshape(4, panels, nodes)
        .transpose(1, 0, 2)
        .reshape(panels, width)
    )
    ids1 = (crevice_centre.T.reshape(pairs) + 1).reshape(fanout, panels)
    destination = crevice_routes.T.reshape(pairs)
    slot_index = destination * capacity + route_rank(destination, devices)
    slot_t = slot_index.reshape(fanout, panels)
    extra = [ids1[t] // 16 for t in range(fanout)] + [ids1[t] % 16 for t in range(fanout)]
    extra += [slot_t[t] // 64 for t in range(fanout)] + [slot_t[t] % 64 for t in range(fanout)]
    rhs = jnp.concatenate([split3(coarse, 1), jnp.stack(extra, axis=1).astype(BF)], axis=1)
    slot_iota = jnp.arange(slots, dtype=jnp.int32)[:, None]
    place = functools.reduce(jnp.logical_or, [slot_iota == slot_t[t][None, :] for t in range(fanout)]).astype(BF)
    placed = jnp.dot(place, rhs, preferred_element_type=F32)
    payload = join3(placed[:, : 3 * width], 1)
    col = 3 * width
    slot_here = jnp.arange(slots, dtype=F32)
    slot_ids = jnp.zeros((slots,), F32)
    for t in range(fanout):
        id_t = 16.0 * placed[:, col + t] + placed[:, col + fanout + t]
        slot_of_t = 64.0 * placed[:, col + 2 * fanout + t] + placed[:, col + 3 * fanout + t]
        slot_ids = jnp.where(slot_of_t == slot_here, id_t, slot_ids)
    outgoing = jnp.concatenate(
        [
            payload.reshape(devices, capacity * width),
            slot_ids.reshape(devices, capacity),
            jnp.zeros((devices, 2 * width - capacity), F32),
        ],
        axis=1,
    )

    incoming = lax.all_to_all(outgoing, ("grp", "dev"), split_axis=0, concat_axis=0, tiled=True)

    rows = capacity // 2
    block = incoming.reshape(devices, rows + 1, 2 * width)
    coarse_in = block[:, :rows, :].reshape(slots // 2, 2 * width)
    ids = jnp.round(block[:, rows, :capacity]).astype(jnp.int32)
    ids = ids.reshape(devices, rows, 2).transpose(2, 0, 1).reshape(2, slots // 2) - 1
    valid = ids >= 0
    pick = (jnp.arange(centre_count, dtype=jnp.int32)[None, :, None] == ids[:, None, :]).astype(BF)

    rel = targets.reshape(3, centre_count, nodes) - centres[:, :, None]
    data_rows = 3 + 3 * nodes
    padded_rows = -(-data_rows // 8) * 8
    centre_data = jnp.concatenate(
        [
            centres,
            rel.transpose(0, 2, 1).reshape(3 * nodes, centre_count),
            jnp.zeros((padded_rows - data_rows, centre_count), F32),
        ],
        axis=0,
    )
    gathered = join2(jnp.einsum("fg,pgs->pfs", split2(centre_data, 0), pick, preferred_element_type=F32), 1)
    slot_centre = gathered[:, :3]
    slot_targets = gathered[:, 3:data_rows].reshape(2, 3, nodes, slots // 2)

    eye_c = jnp.eye(4, dtype=F32)
    eye_p = jnp.eye(2, dtype=F32)
    refine_w = (
        eye_p[:, None, None, :, None, None] * eye_c[None, :, None, None, :, None] * upsample[None, None, :, None, None, :]
    ).reshape(2 * 4 * fine_count, 2 * width)
    upper = lax.dot_general(refine_w, coarse_in, (((1,), (1,)), ((), ())), precision=lax.Precision.HIGH)
    upper = upper.reshape(2, 4, fine_count, slots // 2)
    strength = upper[:, 3] * fine_weights[None, :, None]
    terms = expansion_terms(upper[:, :3], strength, slot_centre, slot_targets)
    terms = jnp.where(valid[:, None, :], terms, 0.0)

    potential = join2(jnp.einsum("pks,pgs->kg", split2(terms, 1), pick, preferred_element_type=F32), 0)

    home = centre_home.reshape(-1)
    back_index = home * capacity_back + route_rank(home, devices)
    back_place = (
        jnp.arange(devices * capacity_back, dtype=jnp.int32)[:, None] == back_index[None, :]
    ).astype(BF)
    sending = join3(
        lax.dot_general(back_place, split3(potential, 0), (((1,), (1,)), ((), ())), preferred_element_type=F32), 1
    )
    sending = sending.reshape(devices, capacity_back * nodes)
    returned = lax.all_to_all(sending, ("grp", "dev"), split_axis=0, concat_axis=0, tiled=True)
    return returned.reshape(-1)


def solution(mesh):
    placed = (
        P(None, ("grp", "dev")),
        P(("grp", "dev")),
        P(("grp", "dev"), None),
        P(("grp", "dev"), None),
        P(None, ("grp", "dev")),
        P(None, ("grp", "dev")),
        P(("grp", "dev"), None),
        P(),
        P(),
    )
    return jax.shard_map(
        per_device, mesh=mesh, in_specs=placed, out_specs=P(("grp", "dev")), check_vma=False
    )
```

```python
import jax
import jax.numpy as jnp
from jax import lax
from jax.sharding import PartitionSpec as P

ORDER = 8
HI = lax.Precision.HIGHEST
BF = jnp.bfloat16
F32 = jnp.float32


def route_rank(destination, count):
    rows = destination.shape[0]
    block = 128 if rows % 128 == 0 else rows
    onehot = (destination[:, None] == jnp.arange(count, dtype=jnp.int32)[None, :]).astype(BF)
    onehot = onehot.reshape(rows // block, block, count)
    lower = (jnp.arange(block)[:, None] > jnp.arange(block)[None, :]).astype(BF)
    within = jnp.einsum("ij,bjc->bic", lower, onehot, preferred_element_type=F32)
    totals = jnp.sum(onehot.astype(F32), axis=1)
    earlier = (jnp.arange(rows // block)[:, None] > jnp.arange(rows // block)[None, :]).astype(F32)
    offsets = jnp.dot(earlier, totals, precision=HI)
    before = within + offsets[:, None, :]
    return jnp.sum(before * onehot.astype(F32), axis=2).reshape(rows).astype(jnp.int32)


def split3(x, axis):
    hi = lax.reduce_precision(x, exponent_bits=8, mantissa_bits=7)
    rest = x - hi
    mid = lax.reduce_precision(rest, exponent_bits=8, mantissa_bits=7)
    lo = rest - mid
    return jnp.concatenate([hi, mid, lo], axis=axis).astype(BF)


def split2(x, axis):
    hi = lax.reduce_precision(x, exponent_bits=8, mantissa_bits=7)
    return jnp.concatenate([hi, x - hi], axis=axis).astype(BF)


def join2(y, axis):
    a, b = jnp.split(y, 2, axis=axis)
    return a + b


def join3(y, axis):
    a, b, c = jnp.split(y, 3, axis=axis)
    return (a + b) + c


def clenshaw_constants(order):
    c1 = [(2 * l + 1) / (l + 1) for l in range(order + 1)]
    c2 = [l / (l + 1) for l in range(order + 2)]
    mu = [1.0] * (order + 1)
    for l in range(order - 1, -1, -1):
        mu[l] = c1[l] * mu[l + 1]
    gamma = [c2[l + 1] / (c1[l] * c1[l + 1]) for l in range(order - 1)]
    return mu, gamma


def expansion_terms(fine, strength, centre_pos, rel_targets):
    mu, gamma = clenshaw_constants(ORDER)
    ax = fine[:, 0] - centre_pos[:, 0][:, None]
    ay = fine[:, 1] - centre_pos[:, 1][:, None]
    az = fine[:, 2] - centre_pos[:, 2][:, None]
    bx, by, bz = rel_targets[:, 0], rel_targets[:, 1], rel_targets[:, 2]
    rs2 = ax * ax + ay * ay + az * az
    rt2 = bx * bx + by * by + bz * bz
    inv_rs2 = 1.0 / rs2
    scale = (strength * mu[0]) * lax.rsqrt(rs2)
    ax = ax * inv_rs2
    ay = ay * inv_rs2
    az = az * inv_rs2
    w = ax[:, :, None] * bx[:, None] + ay[:, :, None] * by[:, None] + az[:, :, None] * bz[:, None]
    rho2 = rt2[:, None] * inv_rs2[:, :, None]
    t_next = w + (1.0 / mu[ORDER - 1])
    t_after = jnp.ones_like(w)
    for level in range(ORDER - 2, -1, -1):
        t_now = (w * t_next + (1.0 / mu[level])) - gamma[level] * (rho2 * t_after)
        t_after, t_next = (t_next, t_now)
    return jnp.sum(scale[:, :, None] * t_next, axis=1)


def per_device(
    panel_nodes,
    density,
    crevice_routes,
    crevice_centre,
    centres,
    targets,
    centre_home,
    upsample,
    fine_weights,
):
    devices = lax.axis_size(("grp", "dev"))
    panels = crevice_routes.shape[0]
    fanout = crevice_routes.shape[1]
    centre_count = centres.shape[1]
    capacity = max(2, 2 * panels * fanout // devices)
    capacity_back = max(2, 2 * centre_count // devices)
    fine_count, nodes = upsample.shape
    pairs = panels * fanout
    slots = devices * capacity
    width = 4 * nodes

    coarse = (
        lax.optimization_barrier(jnp.concatenate([panel_nodes, density[None]], axis=0))
        .reshape(4, panels, nodes)
        .transpose(1, 0, 2)
        .reshape(panels, width)
    )
    coarse_parts = jnp.concatenate([split3(coarse, 1)] * fanout, axis=0)
    ids1 = crevice_centre.T.reshape(pairs) + 1
    id_parts = jnp.stack([ids1 // 16, ids1 % 16], axis=1).astype(BF)
    rhs = jnp.concatenate([coarse_parts, id_parts], axis=1)

    destination = crevice_routes.T.reshape(pairs)
    slot_index = destination * capacity + route_rank(destination, devices)
    place = (jnp.arange(slots, dtype=jnp.int32)[:, None] == slot_index[None, :]).astype(BF)
    placed = jnp.dot(place, rhs, preferred_element_type=F32)
    payload = join3(placed[:, : 3 * width], 1)
    slot_ids = 16.0 * placed[:, 3 * width] + placed[:, 3 * width + 1]
    outgoing = jnp.concatenate(
        [
            payload.reshape(devices, capacity * width),
            slot_ids.reshape(devices, capacity),
            jnp.zeros((devices, 2 * width - capacity), F32),
        ],
        axis=1,
    )

    incoming = lax.all_to_all(outgoing, ("grp", "dev"), split_axis=0, concat_axis=0, tiled=True)

    rows = capacity // 2
    block = incoming.reshape(devices, rows + 1, 2 * width)
    coarse_in = block[:, :rows, :].reshape(slots // 2, 2 * width)
    ids = jnp.round(block[:, rows, :capacity]).astype(jnp.int32)
    ids = ids.reshape(devices, rows, 2).transpose(2, 0, 1).reshape(2, slots // 2) - 1
    valid = ids >= 0
    pick = (jnp.arange(centre_count, dtype=jnp.int32)[None, :, None] == ids[:, None, :]).astype(BF)

    rel = targets.reshape(3, centre_count, nodes) - centres[:, :, None]
    data_rows = 3 + 3 * nodes
    padded_rows = -(-data_rows // 8) * 8
    centre_data = jnp.concatenate(
        [
            centres,
            rel.transpose(0, 2, 1).reshape(3 * nodes, centre_count),
            jnp.zeros((padded_rows - data_rows, centre_count), F32),
        ],
        axis=0,
    )
    gathered = join2(jnp.einsum("fg,pgs->pfs", split2(centre_data, 0), pick, preferred_element_type=F32), 1)
    slot_centre = gathered[:, :3]
    slot_targets = gathered[:, 3:data_rows].reshape(2, 3, nodes, slots // 2)

    eye_c = jnp.eye(4, dtype=F32)
    eye_p = jnp.eye(2, dtype=F32)
    refine_w = (
        eye_p[:, None, None, :, None, None] * eye_c[None, :, None, None, :, None] * upsample[None, None, :, None, None, :]
    ).reshape(2 * 4 * fine_count, 2 * width)
    upper = lax.dot_general(refine_w, coarse_in, (((1,), (1,)), ((), ())), precision=lax.Precision.HIGH)
    upper = upper.reshape(2, 4, fine_count, slots // 2)
    strength = upper[:, 3] * fine_weights[None, :, None]
    terms = expansion_terms(upper[:, :3], strength, slot_centre, slot_targets)
    terms = jnp.where(valid[:, None, :], terms, 0.0)

    potential = join2(jnp.einsum("pks,pgs->kg", split2(terms, 1), pick, preferred_element_type=F32), 0)

    home = centre_home.reshape(-1)
    back_index = home * capacity_back + route_rank(home, devices)
    back_place = (
        jnp.arange(devices * capacity_back, dtype=jnp.int32)[:, None] == back_index[None, :]
    ).astype(BF)
    sending = join3(
        lax.dot_general(back_place, split3(potential, 0), (((1,), (1,)), ((), ())), preferred_element_type=F32), 1
    )
    sending = sending.reshape(devices, capacity_back * nodes)
    returned = lax.all_to_all(sending, ("grp", "dev"), split_axis=0, concat_axis=0, tiled=True)
    return returned.reshape(-1)


def solution(mesh):
    placed = (
        P(None, ("grp", "dev")),
        P(("grp", "dev")),
        P(("grp", "dev"), None),
        P(("grp", "dev"), None),
        P(None, ("grp", "dev")),
        P(None, ("grp", "dev")),
        P(("grp", "dev"), None),
        P(),
        P(),
    )
    return jax.shard_map(
        per_device, mesh=mesh, in_specs=placed, out_specs=P(("grp", "dev")), check_vma=False
    )
```
